512 devices in a mesh: mesh: 128 (over z, y, core), inner: 4 (over x).
Axes of the slice: x: 4, y: 4, z: 16, core: 2. Of those that a mesh axis runs over, the one named last changes fastest.
Arguments:
- source: float32 [64, 131072], P(None, ('mesh', 'inner')), may hold values from -8 to 8
- density: float32 [131072], P(('mesh', 'inner')), may hold values from 0.1 to 1
- neighbours: int32 [6, 131072], P(None, ('mesh', 'inner')), may hold values from 0 to 512, as said below
- halo_sends: int32 [2, 65536], P(None, ('mesh', 'inner')), may hold values from 0 to 255, as said below
- aggregate: int32 [131072], P(('mesh', 'inner')), may hold values from 0 to 31, as said below
- partner_map: int32 [512, 64], replicated, may hold values from 0 to 31, as said below
Outputs:
- correction: float32 [64, 131072], P(None, ('mesh', 'inner'))
- coarse_correction: float32 [131072], P(('mesh', 'inner'))
The draws below stay inside these ranges and needn't reach their ends.
Inputs may be any that keep to these rules, and one draw needn't show every extreme that they name: Each device's elements are a brick of 16 x 8 x 2 elements in a drawn order; devices follow each other along z. Values below 256 are local elements, neighbours are mutual through opposite faces; only the -z face points into the rim from below and only the +z face into the rim from above, at slot x * 8 + y of the element's position; x and y walls get 256 + 2 * 128, as do no others. `halo_sends`: row 0 of a device lists its bottom z layer, row 1 its top z layer, each in the order x * 8 + y of the elements' positions, as local element numbers. Each aggregate is a 2 x 2 x 2 block of elements of the brick; each value occurs exactly 8 times on each device. `partner_map`: every row gives each of 64 children its parent; each parent has exactly two children. The last row is the only one that no level names.
All inputs are finite; a program needn't handle non-finite values.
Results may differ from the reference program's by a relative error of at most 0.0001.
Values sent between devices are 32-bit elements; how exact they have to be, the bound alone decides.
No kernel may reach another device: no remote copies, remote signals or barrier semaphores. Data moves between devices by JAX's collectives and lax.ppermute only.
A program may use at most 64 MiB of HBM per device.

```python
import math
from functools import partial
import jax
import jax.numpy as jnp
import numpy as np
from jax import lax

BX = 16
BY = 8
BZ = 2
NODES = 64
SMOOTH_FINE = 3
SMOOTH_LIN = 2
E_DEV = 256
H = 128
G = 32
E_TOTAL = 131072
N_MESH = 128
N_INNER = 4


def mesh_layout(key):
    devices = E_TOTAL // E_DEV
    elements = BX * BY * BZ
    layer = BX * BY
    device_keys = jax.random.split(jax.random.fold_in(key, 11), devices)

    def one_order(one_key):
        return jax.random.permutation(one_key, elements).astype(jnp.int32)
    orders = jax.vmap(one_order)(device_keys)
    position = jnp.arange(elements, dtype=jnp.int32)
    pos_x = position // BY % BX
    pos_y = position % BY
    pos_z = position // layer
    wall_slot = elements + 2 * layer

    def one_device(ordering):

        def moved(offset):
            return ordering[jnp.clip(position + offset, 0, elements - 1)]
        values = jnp.stack([jnp.where(pos_x > 0, moved(-BY), wall_slot), jnp.where(pos_x < BX - 1, moved(BY), wall_slot), jnp.where(pos_y > 0, moved(-1), wall_slot), jnp.where(pos_y < BY - 1, moved(1), wall_slot), jnp.where(pos_z > 0, moved(-layer), elements + position % layer), jnp.where(pos_z < BZ - 1, moved(layer), elements + layer + position % layer)]).astype(jnp.int32)
        face_table = jnp.zeros((6, elements), jnp.int32).at[:, ordering].set(values)
        groups = ((pos_z // 2 * (BX // 2) + pos_x // 2) * (BY // 2) + pos_y // 2).astype(jnp.int32)
        agg_ids = jnp.zeros((elements,), jnp.int32).at[ordering].set(groups)
        send_rows = jnp.stack([ordering[:layer], ordering[elements - layer:]])
        return (face_table, agg_ids, send_rows)
    return jax.vmap(one_device)(orders)


def draw_neighbours(key, part):
    face_table, agg_ids, send_rows = mesh_layout(key)
    return face_table.transpose(1, 0, 2).reshape(6, E_TOTAL)


def draw_halo_sends(key, part):
    face_table, agg_ids, send_rows = mesh_layout(key)
    devices = E_TOTAL // E_DEV
    return send_rows.transpose(1, 0, 2).reshape(2, devices * BX * BY)


def draw_aggregate(key, part):
    face_table, agg_ids, send_rows = mesh_layout(key)
    return agg_ids.reshape(E_TOTAL)


def draw_partner_map(key, part):
    devices = E_TOTAL // E_DEV
    children = 2 * (E_DEV // 8)

    def one_row(row_id):
        row_key = jax.random.fold_in(jax.random.fold_in(key, 29), row_id)
        ordering = jax.random.permutation(row_key, children).astype(jnp.int32)
        return jnp.zeros((children,), jnp.int32).at[ordering].set(jnp.arange(children, dtype=jnp.int32) // 2)
    return jax.vmap(one_row)(jnp.arange(devices, dtype=jnp.int32))


def draw_source(key, part):
    shape = (NODES, E_TOTAL)
    return jnp.clip(2.0 * jax.random.normal(key, shape, jnp.float32), -8.0, 8.0)


def block_scale(rng, dims, pieces, least, top_value):
    loudness = 1.0
    for dim, shards_of in pieces:
        heights = jax.random.uniform(jax.random.fold_in(jax.random.fold_in(rng, 6), dim), (shards_of,), jnp.float32, least / len(pieces), top_value / len(pieces))
        loudness = loudness * jnp.repeat(jnp.exp(heights), dims[dim] // shards_of).reshape((-1,) + (1,) * (len(dims) - 1 - dim))
    return loudness


def setup_inputs(seed: int = 0) -> dict:
    seeds = jax.random.split(jax.random.key(seed), 7)
    source = draw_source(jax.random.fold_in(seeds[6], 71), 0)
    density = jnp.clip(jnp.exp(math.log(1.0) - 2.3025851 * jax.random.uniform(seeds[1], (E_TOTAL,), jnp.float32) ** block_scale(seeds[1], (E_TOTAL,), ((0, 512),), -0.2, 0.2)), 0.1, 1.0)
    neighbours = draw_neighbours(jax.random.fold_in(seeds[6], 71), 0)
    halo_sends = draw_halo_sends(jax.random.fold_in(seeds[6], 71), 0)
    aggregate = draw_aggregate(jax.random.fold_in(seeds[6], 71), 0)
    partner_map = draw_partner_map(jax.random.fold_in(seeds[6], 71), 0)
    return {"source": source, "density": density, "neighbours": neighbours, "halo_sends": halo_sends, "aggregate": aggregate, "partner_map": partner_map}


PENALTY = 2.0
FINE_WEIGHT = 0.6
LINEAR_WEIGHT = 0.5
PRECISE = lax.Precision.HIGHEST


def main_diagonal(matrix):
    positions = np.arange(matrix.shape[0])
    return matrix[positions, positions]


def build_tables():
    line_stiff = np.array([[1.0, -1.0, 0.0, 0.0], [-1.0, 2.0, -1.0, 0.0], [0.0, -1.0, 2.0, -1.0], [0.0, 0.0, -1.0, 1.0]])
    identity = np.eye(4)
    stiffness = np.kron(np.kron(line_stiff, identity), identity) + np.kron(np.kron(identity, line_stiff), identity) + np.kron(np.kron(identity, identity), line_stiff)
    ramp_basis = np.array([[1.0, 0.0], [2.0 / 3.0, 1.0 / 3.0], [1.0 / 3.0, 2.0 / 3.0], [0.0, 1.0]])
    prolong = np.kron(np.kron(ramp_basis, ramp_basis), ramp_basis)
    coarse_stiff = prolong.T @ stiffness @ prolong
    small_mass = ramp_basis.T @ ramp_basis
    face_mass = np.kron(small_mass, small_mass)
    return stiffness, prolong, coarse_stiff, face_mass


def face_slices(points):
    grid_ids = np.arange(points ** 3).reshape(points, points, points)
    last_index = points - 1
    return [grid_ids[0], grid_ids[last_index], grid_ids[:, 0], grid_ids[:, last_index], grid_ids[:, :, 0], grid_ids[:, :, last_index]]


def lifting(points, face_mat):
    node_total = points ** 3
    per_face = points * points
    slices = face_slices(points)
    result = np.zeros((node_total, 6 * per_face))
    for face in range(6):
        select = np.zeros((node_total, per_face))
        select[slices[face].ravel(), np.arange(per_face)] = 1.0
        result[:, face * per_face:(face + 1) * per_face] = PENALTY * (select @ face_mat)
    return result


def face_diagonal(points, face_mat):
    result = np.zeros(points ** 3)
    for face_ids in face_slices(points):
        result[face_ids.ravel()] += PENALTY * main_diagonal(face_mat)
    return result


def face_values(nodal_field, points):
    cube_view = nodal_field.reshape(points, points, points, -1)
    last_index = points - 1
    slices = [cube_view[0], cube_view[last_index], cube_view[:, 0], cube_view[:, last_index], cube_view[:, :, 0], cube_view[:, :, last_index]]
    return [piece.reshape(points * points, -1) for piece in slices]


def apply_level(nodal_field, local_density, local_neighbours, rim_low, rim_high, stiff, lifting_mat, points):
    traces = face_values(nodal_field, points)
    wall_zero = jnp.zeros((points * points, 1), jnp.float32)
    jump_list = []
    for face in range(6):
        extended = jnp.concatenate([traces[face ^ 1], rim_low, rim_high, wall_zero], axis=1)
        jump_list.append(traces[face] - jnp.take(extended, local_neighbours[face], axis=1))
    jumps = jnp.concatenate(jump_list, axis=0)
    inner_part = local_density[None, :] * jnp.dot(stiff, nodal_field, precision=PRECISE)
    return inner_part + jnp.dot(lifting_mat, jumps, precision=PRECISE)


def scale_of(level):
    return 96.0 * PENALTY * (8.0 * 2.0 ** level) ** (2.0 / 3.0)


def climb(block, partner_map, first):
    groups_width = block.shape[1]
    sums = [block]
    rows = []
    current = block
    level = first

    def merge_one(values, parent_ids):
        return jax.ops.segment_sum(values, parent_ids, num_segments=groups_width)

    while current.shape[0] > 1:
        level += 1
        halves = current.shape[0] // 2
        row_ids = jnp.arange(halves, dtype=jnp.int32) * (2 ** level) + (2 ** (level - 1) - 1)
        parents = jnp.take(partner_map, row_ids, axis=0)
        current = jax.vmap(merge_one)(current.reshape(halves, 2 * groups_width), parents)
        sums.append(current)
        rows.append(parents)
    total = sums[-1] / scale_of(level)
    for depth in range(len(rows) - 1, -1, -1):
        children = jnp.take_along_axis(total, rows[depth], axis=1)
        total = children.reshape(-1, groups_width) + sums[depth] / scale_of(first + depth)
    return total


def reference(source, density, neighbours, halo_sends, aggregate, partner_map):
    devices = N_MESH * N_INNER
    elements = E_DEV
    rim_width = H
    groups_width = G
    stiffness, prolong, coarse_stiff, face_mass = build_tables()
    stiff_fine = jnp.asarray(stiffness, jnp.float32)
    stiff_lin = jnp.asarray(coarse_stiff, jnp.float32)
    prolong_mat = jnp.asarray(prolong, jnp.float32)
    lift_fine = jnp.asarray(lifting(4, np.eye(16)), jnp.float32)
    lift_lin = jnp.asarray(lifting(2, face_mass), jnp.float32)
    diag_fine_k = jnp.asarray(main_diagonal(stiffness), jnp.float32)
    diag_fine_f = jnp.asarray(face_diagonal(4, np.eye(16)), jnp.float32)
    diag_lin_k = jnp.asarray(main_diagonal(coarse_stiff), jnp.float32)
    diag_lin_f = jnp.asarray(face_diagonal(2, face_mass), jnp.float32)

    rhs = source.reshape(NODES, devices, elements).transpose(1, 0, 2)
    local_density = density.reshape(devices, elements)
    local_neighbours = neighbours.reshape(6, devices, elements).transpose(1, 0, 2)
    send_rows = halo_sends.reshape(2, devices, rim_width).transpose(1, 0, 2)
    agg_ids = aggregate.reshape(devices, elements)

    diag_fine = local_density[:, None, :] * diag_fine_k[None, :, None] + diag_fine_f[None, :, None]
    diag_lin = local_density[:, None, :] * diag_lin_k[None, :, None] + diag_lin_f[None, :, None]

    def rims(fields, points):
        def outgoing(nodal_field, sends):
            traces = face_values(nodal_field, points)
            return jnp.take(traces[5], sends[1], axis=1), jnp.take(traces[4], sends[0], axis=1)

        upward, downward = jax.vmap(outgoing)(fields, send_rows)
        zero_rim = jnp.zeros_like(upward[:1])
        rim_low = jnp.concatenate([zero_rim, upward[:-1]], axis=0)
        rim_high = jnp.concatenate([downward[1:], zero_rim], axis=0)
        return rim_low, rim_high

    def apply_fine(fields):
        rim_low, rim_high = rims(fields, 4)
        return jax.vmap(partial(apply_level, stiff=stiff_fine, lifting_mat=lift_fine, points=4))(fields, local_density, local_neighbours, rim_low, rim_high)

    def apply_lin(fields):
        rim_low, rim_high = rims(fields, 2)
        return jax.vmap(partial(apply_level, stiff=stiff_lin, lifting_mat=lift_lin, points=2))(fields, local_density, local_neighbours, rim_low, rim_high)

    def batch_dot(matrix, fields):
        return jax.vmap(lambda one: jnp.dot(matrix, one, precision=PRECISE))(fields)

    solution = FINE_WEIGHT * rhs / diag_fine
    for sweep in range(SMOOTH_FINE - 1):
        solution = solution + FINE_WEIGHT * (rhs - apply_fine(solution)) / diag_fine
    resid_fine = rhs - apply_fine(solution)
    resid_lin = batch_dot(prolong_mat.T, resid_fine)
    linear = LINEAR_WEIGHT * resid_lin / diag_lin
    for sweep in range(SMOOTH_LIN - 1):
        linear = linear + LINEAR_WEIGHT * (resid_lin - apply_lin(linear)) / diag_lin
    left_lin = resid_lin - apply_lin(linear)
    resid_elem = jnp.sum(left_lin, axis=1)

    def agg_sum(values, ids):
        return jax.ops.segment_sum(values, ids, num_segments=groups_width)

    agg_sums = jax.vmap(agg_sum)(resid_elem, agg_ids)
    agg_total = climb(agg_sums, partner_map, 0)
    coarse = resid_elem / (96.0 * PENALTY) + jnp.take_along_axis(agg_total, agg_ids, axis=1)
    linear = linear + coarse[:, None, :]
    for sweep in range(SMOOTH_LIN):
        linear = linear + LINEAR_WEIGHT * (resid_lin - apply_lin(linear)) / diag_lin
    solution = solution + batch_dot(prolong_mat, linear)
    for sweep in range(SMOOTH_FINE):
        solution = solution + FINE_WEIGHT * (rhs - apply_fine(solution)) / diag_fine
    correction = solution.transpose(1, 0, 2).reshape(NODES, devices * elements)
    return correction, coarse.reshape(devices * elements)
```

```python
import jax
import jax.numpy as jnp
import numpy as np
from jax import lax
from jax.sharding import PartitionSpec as P

SMOOTH_FINE = 3
SMOOTH_LIN = 2
BRICK_Y = 8

PENALTY = 2.0
FINE_WEIGHT = 0.6
LINEAR_WEIGHT = 0.5
PRECISE = lax.Precision.HIGHEST
AXES = ("mesh", "inner")


def shifted(value, axis, steps):
    count = lax.axis_size(axis)
    leading, last = (max(0, -steps), min(count, count - steps))
    return lax.ppermute(value, axis, [(source, source + steps) for source in range(leading, last)])


def main_diagonal(matrix):
    positions = np.arange(matrix.shape[0])
    return matrix[positions, positions]


def build_tables():
    line_stiff = np.array(
        [
            [1.0, -1.0, 0.0, 0.0],
            [-1.0, 2.0, -1.0, 0.0],
            [0.0, -1.0, 2.0, -1.0],
            [0.0, 0.0, -1.0, 1.0],
        ]
    )
    identity = np.eye(4)
    stiffness = (
        np.kron(np.kron(line_stiff, identity), identity)
        + np.kron(np.kron(identity, line_stiff), identity)
        + np.kron(np.kron(identity, identity), line_stiff)
    )
    ramp_basis = np.array([[1.0, 0.0], [2.0 / 3.0, 1.0 / 3.0], [1.0 / 3.0, 2.0 / 3.0], [0.0, 1.0]])
    prolong = np.kron(np.kron(ramp_basis, ramp_basis), ramp_basis)
    coarse_stiff = prolong.T @ stiffness @ prolong
    small_mass = ramp_basis.T @ ramp_basis
    face_mass = np.kron(small_mass, small_mass)
    return (stiffness, prolong, coarse_stiff, face_mass)


def face_slices(points):
    grid_ids = np.arange(points**3).reshape(points, points, points)
    last_index = points - 1
    return [
        grid_ids[0],
        grid_ids[last_index],
        grid_ids[:, 0],
        grid_ids[:, last_index],
        grid_ids[:, :, 0],
        grid_ids[:, :, last_index],
    ]


def lifting(points, face_mat):
    node_total = points**3
    per_face = points * points
    slices = face_slices(points)
    result = np.zeros((node_total, 6 * per_face))
    for face in range(6):
        select = np.zeros((node_total, per_face))
        select[slices[face].ravel(), np.arange(per_face)] = 1.0
        result[:, face * per_face : (face + 1) * per_face] = PENALTY * (select @ face_mat)
    return result


def face_diagonal(points, face_mat):
    result = np.zeros(points**3)
    for face_ids in face_slices(points):
        result[face_ids.ravel()] += PENALTY * main_diagonal(face_mat)
    return result


def stiff_and_traces(stiff, points):
    node_total = points**3
    per_face = points * points
    select = np.zeros((6 * per_face, node_total))
    for face, ids in enumerate(face_slices(points)):
        select[face * per_face + np.arange(per_face), ids.ravel()] = 1.0
    return np.concatenate([stiff, select], axis=0)


def shift_columns(values, offset):
    rows, width = values.shape
    pad = jnp.zeros((rows, abs(offset)), values.dtype)
    if offset > 0:
        return jnp.concatenate([values[:, offset:], pad], axis=1)
    return jnp.concatenate([pad, values[:, : width + offset]], axis=1)


def scale_of(level):
    return 96.0 * PENALTY * (8.0 * 2.0**level) ** (2.0 / 3.0)


def local(source, density, neighbours, halo_sends, aggregate, partner_map):
    stiffness, prolong, coarse_stiff, face_mass = build_tables()
    big_fine = jnp.asarray(stiff_and_traces(stiffness, 4), jnp.float32)
    big_lin = jnp.asarray(stiff_and_traces(coarse_stiff, 2), jnp.float32)
    prolong_mat = jnp.asarray(prolong, jnp.float32)
    lift_fine = jnp.asarray(lifting(4, np.eye(16)), jnp.float32)
    lift_lin = jnp.asarray(lifting(2, face_mass), jnp.float32)
    diag_fine_k = jnp.asarray(main_diagonal(stiffness), jnp.float32)
    diag_fine_f = jnp.asarray(face_diagonal(4, np.eye(16)), jnp.float32)
    diag_lin_k = jnp.asarray(main_diagonal(coarse_stiff), jnp.float32)
    diag_lin_f = jnp.asarray(face_diagonal(2, face_mass), jnp.float32)
    elements = source.shape[1]
    layer = halo_sends.shape[1]
    groups_width = elements // 8

    ordering = jnp.concatenate([halo_sends[0], halo_sends[1]])
    inverse = jnp.zeros((elements,), jnp.int32).at[ordering].set(
        jnp.arange(elements, dtype=jnp.int32)
    )
    rhs = jnp.take(source, ordering, axis=1)
    dens = jnp.take(density, ordering)
    agg = jnp.take(aggregate, ordering)

    column = np.arange(elements)
    pos_x = column % layer // BRICK_Y
    pos_y = column % BRICK_Y
    last_x = layer // BRICK_Y - 1
    masks = [
        jnp.asarray(pos_x > 0),
        jnp.asarray(pos_x < last_x),
        jnp.asarray(pos_y > 0),
        jnp.asarray(pos_y < BRICK_Y - 1),
    ]
    offsets = [-BRICK_Y, BRICK_Y, -1, 1]

    diag_fine = dens[None, :] * diag_fine_k[:, None] + diag_fine_f[:, None]
    diag_lin = dens[None, :] * diag_lin_k[:, None] + diag_lin_f[:, None]

    def apply(nodal_field, big, lift, node_total, per_face):
        stacked = jnp.dot(big, nodal_field, precision=PRECISE)
        stiff_part = stacked[:node_total]
        traces = [
            stacked[node_total + f * per_face : node_total + (f + 1) * per_face] for f in range(6)
        ]
        rim_low = shifted(traces[5][:, layer:], AXES, 1)
        rim_high = shifted(traces[4][:, :layer], AXES, -1)
        jumps = []
        for face in range(4):
            other = shift_columns(traces[face ^ 1], offsets[face])
            jumps.append(traces[face] - jnp.where(masks[face][None, :], other, 0.0))
        jumps.append(traces[4] - jnp.concatenate([rim_low, traces[5][:, :layer]], axis=1))
        jumps.append(traces[5] - jnp.concatenate([traces[4][:, layer:], rim_high], axis=1))
        jumps = jnp.concatenate(jumps, axis=0)
        return dens[None, :] * stiff_part + jnp.dot(lift, jumps, precision=PRECISE)

    def apply_fine(nodal_field):
        return apply(nodal_field, big_fine, lift_fine, 64, 16)

    def apply_lin(nodal_field):
        return apply(nodal_field, big_lin, lift_lin, 8, 4)

    solution = FINE_WEIGHT * rhs / diag_fine
    for sweep in range(SMOOTH_FINE - 1):
        solution = solution + FINE_WEIGHT * (rhs - apply_fine(solution)) / diag_fine
    resid_fine = rhs - apply_fine(solution)
    resid_lin = jnp.dot(prolong_mat.T, resid_fine, precision=PRECISE)
    linear = LINEAR_WEIGHT * resid_lin / diag_lin
    for sweep in range(SMOOTH_LIN - 1):
        linear = linear + LINEAR_WEIGHT * (resid_lin - apply_lin(linear)) / diag_lin
    left_lin = resid_lin - apply_lin(linear)
    resid_elem = jnp.sum(left_lin, axis=0)

    group_ids = jnp.arange(groups_width, dtype=jnp.int32)
    agg_hot = agg[:, None] == group_ids[None, :]
    own_sums = jnp.sum(jnp.where(agg_hot, resid_elem[:, None], 0.0), axis=0)

    current = lax.all_gather(own_sums, AXES)
    sums = [current]
    hots = []
    level = 0
    while current.shape[0] > 1:
        level += 1
        halves = current.shape[0] // 2
        parents = partner_map.reshape(halves, 2**level, 2 * groups_width)[:, 2 ** (level - 1) - 1]
        hot = parents[:, :, None] == group_ids[None, None, :]
        paired = current.reshape(halves, 2 * groups_width)
        current = jnp.sum(jnp.where(hot, paired[:, :, None], 0.0), axis=1)
        sums.append(current)
        hots.append(hot)
    total = sums[-1] / scale_of(level)
    for depth in range(len(hots) - 1, -1, -1):
        children = jnp.sum(jnp.where(hots[depth], total[:, None, :], 0.0), axis=2)
        total = children.reshape(-1, groups_width) + sums[depth] / scale_of(depth)
    flat_index = lax.axis_index("mesh") * lax.axis_size("inner") + lax.axis_index("inner")
    own_total = lax.dynamic_index_in_dim(total, flat_index, 0, keepdims=False)
    coarse = resid_elem / (96.0 * PENALTY) + jnp.sum(
        jnp.where(agg_hot, own_total[None, :], 0.0), axis=1
    )

    linear = linear + coarse[None, :]
    for sweep in range(SMOOTH_LIN):
        linear = linear + LINEAR_WEIGHT * (resid_lin - apply_lin(linear)) / diag_lin
    solution = solution + jnp.dot(prolong_mat, linear, precision=PRECISE)
    for sweep in range(SMOOTH_FINE):
        solution = solution + FINE_WEIGHT * (rhs - apply_fine(solution)) / diag_fine
    return (jnp.take(solution, inverse, axis=1), jnp.take(coarse, inverse))


def solution(mesh):
    return jax.shard_map(
        local,
        mesh=mesh,
        in_specs=(
            P(None, ("mesh", "inner")),
            P(("mesh", "inner")),
            P(None, ("mesh", "inner")),
            P(None, ("mesh", "inner")),
            P(("mesh", "inner")),
            P(),
        ),
        out_specs=(P(None, ("mesh", "inner")), P(("mesh", "inner"))),
        check_vma=False,
    )
```

```python
import jax
import jax.numpy as jnp
import numpy as np
from jax import lax
from jax.sharding import PartitionSpec as P

SMOOTH_FINE = 3
SMOOTH_LIN = 2
BRICK_Y = 8

PENALTY = 2.0
FINE_WEIGHT = 0.6
LINEAR_WEIGHT = 0.5
PRECISE = lax.Precision.HIGHEST
AXES = ("mesh", "inner")


def shifted(value, axis, steps):
    count = lax.axis_size(axis)
    leading, last = (max(0, -steps), min(count, count - steps))
    return lax.ppermute(value, axis, [(source, source + steps) for source in range(leading, last)])


def main_diagonal(matrix):
    positions = np.arange(matrix.shape[0])
    return matrix[positions, positions]


def build_tables():
    line_stiff = np.array(
        [
            [1.0, -1.0, 0.0, 0.0],
            [-1.0, 2.0, -1.0, 0.0],
            [0.0, -1.0, 2.0, -1.0],
            [0.0, 0.0, -1.0, 1.0],
        ]
    )
    identity = np.eye(4)
    stiffness = (
        np.kron(np.kron(line_stiff, identity), identity)
        + np.kron(np.kron(identity, line_stiff), identity)
        + np.kron(np.kron(identity, identity), line_stiff)
    )
    ramp_basis = np.array([[1.0, 0.0], [2.0 / 3.0, 1.0 / 3.0], [1.0 / 3.0, 2.0 / 3.0], [0.0, 1.0]])
    prolong = np.kron(np.kron(ramp_basis, ramp_basis), ramp_basis)
    coarse_stiff = prolong.T @ stiffness @ prolong
    small_mass = ramp_basis.T @ ramp_basis
    face_mass = np.kron(small_mass, small_mass)
    return (stiffness, prolong, coarse_stiff, face_mass)


def face_slices(points):
    grid_ids = np.arange(points**3).reshape(points, points, points)
    last_index = points - 1
    return [
        grid_ids[0],
        grid_ids[last_index],
        grid_ids[:, 0],
        grid_ids[:, last_index],
        grid_ids[:, :, 0],
        grid_ids[:, :, last_index],
    ]


def lifting(points, face_mat):
    node_total = points**3
    per_face = points * points
    slices = face_slices(points)
    result = np.zeros((node_total, 6 * per_face))
    for face in range(6):
        select = np.zeros((node_total, per_face))
        select[slices[face].ravel(), np.arange(per_face)] = 1.0
        result[:, face * per_face : (face + 1) * per_face] = PENALTY * (select @ face_mat)
    return result


def face_diagonal(points, face_mat):
    result = np.zeros(points**3)
    for face_ids in face_slices(points):
        result[face_ids.ravel()] += PENALTY * main_diagonal(face_mat)
    return result


def stiff_and_traces(stiff, points):
    node_total = points**3
    per_face = points * points
    select = np.zeros((6 * per_face, node_total))
    for face, ids in enumerate(face_slices(points)):
        select[face * per_face + np.arange(per_face), ids.ravel()] = 1.0
    return np.concatenate([stiff, select], axis=0)


def shift_columns(values, offset):
    rows, width = values.shape
    pad = jnp.zeros((rows, abs(offset)), values.dtype)
    if offset > 0:
        return jnp.concatenate([values[:, offset:], pad], axis=1)
    return jnp.concatenate([pad, values[:, : width + offset]], axis=1)


def scale_of(level):
    return 96.0 * PENALTY * (8.0 * 2.0**level) ** (2.0 / 3.0)


def local(source, density, neighbours, halo_sends, aggregate, partner_map):
    stiffness, prolong, coarse_stiff, face_mass = build_tables()
    big_fine = jnp.asarray(stiff_and_traces(stiffness, 4), jnp.float32)
    big_lin = jnp.asarray(stiff_and_traces(coarse_stiff, 2), jnp.float32)
    prolong_mat = jnp.asarray(prolong, jnp.float32)
    lift_fine = jnp.asarray(lifting(4, np.eye(16)), jnp.float32)
    lift_lin = jnp.asarray(lifting(2, face_mass), jnp.float32)
    diag_fine_k = jnp.asarray(main_diagonal(stiffness), jnp.float32)
    diag_fine_f = jnp.asarray(face_diagonal(4, np.eye(16)), jnp.float32)
    diag_lin_k = jnp.asarray(main_diagonal(coarse_stiff), jnp.float32)
    diag_lin_f = jnp.asarray(face_diagonal(2, face_mass), jnp.float32)
    elements = source.shape[1]
    layer = halo_sends.shape[1]
    groups_width = elements // 8

    ordering = jnp.concatenate([halo_sends[0], halo_sends[1]])
    inverse = jnp.zeros((elements,), jnp.int32).at[ordering].set(
        jnp.arange(elements, dtype=jnp.int32)
    )
    rhs = jnp.take(source, ordering, axis=1)
    dens = jnp.take(density, ordering)
    agg = jnp.take(aggregate, ordering)

    column = np.arange(elements)
    pos_x = column % layer // BRICK_Y
    pos_y = column % BRICK_Y
    last_x = layer // BRICK_Y - 1
    masks = [
        jnp.asarray(pos_x > 0),
        jnp.asarray(pos_x < last_x),
        jnp.asarray(pos_y > 0),
        jnp.asarray(pos_y < BRICK_Y - 1),
    ]
    offsets = [-BRICK_Y, BRICK_Y, -1, 1]

    diag_fine = dens[None, :] * diag_fine_k[:, None] + diag_fine_f[:, None]
    diag_lin = dens[None, :] * diag_lin_k[:, None] + diag_lin_f[:, None]

    def apply(nodal_field, big, lift, node_total, per_face):
        stacked = jnp.dot(big, nodal_field, precision=PRECISE)
        stiff_part = stacked[:node_total]
        traces = [
            stacked[node_total + f * per_face : node_total + (f + 1) * per_face] for f in range(6)
        ]
        rim_low = shifted(traces[5][:, layer:], AXES, 1)
        rim_high = shifted(traces[4][:, :layer], AXES, -1)
        jumps = []
        for face in range(4):
            other = shift_columns(traces[face ^ 1], offsets[face])
            jumps.append(traces[face] - jnp.where(masks[face][None, :], other, 0.0))
        jumps.append(traces[4] - jnp.concatenate([rim_low, traces[5][:, :layer]], axis=1))
        jumps.append(traces[5] - jnp.concatenate([traces[4][:, layer:], rim_high], axis=1))
        jumps = jnp.concatenate(jumps, axis=0)
        return dens[None, :] * stiff_part + jnp.dot(lift, jumps, precision=PRECISE)

    def apply_fine(nodal_field):
        return apply(nodal_field, big_fine, lift_fine, 64, 16)

    def apply_lin(nodal_field):
        return apply(nodal_field, big_lin, lift_lin, 8, 4)

    solution = FINE_WEIGHT * rhs / diag_fine
    for sweep in range(SMOOTH_FINE - 1):
        solution = solution + FINE_WEIGHT * (rhs - apply_fine(solution)) / diag_fine
    resid_fine = rhs - apply_fine(solution)
    resid_lin = jnp.dot(prolong_mat.T, resid_fine, precision=PRECISE)
    linear = LINEAR_WEIGHT * resid_lin / diag_lin
    for sweep in range(SMOOTH_LIN - 1):
        linear = linear + LINEAR_WEIGHT * (resid_lin - apply_lin(linear)) / diag_lin
    left_lin = resid_lin - apply_lin(linear)
    resid_elem = jnp.sum(left_lin, axis=0)

    group_ids = jnp.arange(groups_width, dtype=jnp.int32)
    agg_hot = agg[:, None] == group_ids[None, :]
    own_sums = jnp.sum(jnp.where(agg_hot, resid_elem[:, None], 0.0), axis=0)

    flat_index = lax.axis_index("mesh") * lax.axis_size("inner") + lax.axis_index("inner")
    devices = lax.axis_size("mesh") * lax.axis_size("inner")
    top = devices.bit_length() - 1
    current = own_sums
    level = 0
    rounds = []
    while level < top:
        bits = min(3, top - level)
        members = 2**bits
        received = [current] + [
            lax.ppermute(current, AXES, [(i, i ^ (k << level)) for i in range(devices)])
            for k in range(1, members)
        ]
        received = jnp.stack(received)
        own_pos = (flat_index >> level) & (members - 1)
        picks = own_pos ^ jnp.arange(members, dtype=jnp.int32)
        block = jnp.sum(
            jnp.where(
                picks[:, None, None] == jnp.arange(members, dtype=jnp.int32)[None, :, None],
                received[None, :, :],
                0.0,
            ),
            axis=1,
        )
        sums = [block]
        hots = []
        for step in range(1, bits + 1):
            merged_level = level + step
            halves = block.shape[0] // 2
            group = (flat_index >> (level + bits)) * 2 ** (bits - step) + jnp.arange(
                halves, dtype=jnp.int32
            )
            rows = group * 2**merged_level + (2 ** (merged_level - 1) - 1)
            parents = jnp.take(partner_map, rows, axis=0)
            hot = parents[:, :, None] == group_ids[None, None, :]
            paired = block.reshape(halves, 2 * groups_width)
            block = jnp.sum(jnp.where(hot, paired[:, :, None], 0.0), axis=1)
            sums.append(block)
            hots.append(hot)
        rounds.append((level, sums, hots, own_pos))
        current = block[0]
        level += bits
    total = current[None, :] / scale_of(level)
    for base, sums, hots, own_pos in reversed(rounds):
        for step in range(len(hots), 0, -1):
            children = jnp.sum(jnp.where(hots[step - 1], total[:, None, :], 0.0), axis=2)
            total = children.reshape(-1, groups_width) + sums[step - 1] / scale_of(base + step - 1)
        total = lax.dynamic_slice_in_dim(total, own_pos, 1, axis=0)
    own_total = total[0]
    coarse = resid_elem / (96.0 * PENALTY) + jnp.sum(
        jnp.where(agg_hot, own_total[None, :], 0.0), axis=1
    )

    linear = linear + coarse[None, :]
    for sweep in range(SMOOTH_LIN):
        linear = linear + LINEAR_WEIGHT * (resid_lin - apply_lin(linear)) / diag_lin
    solution = solution + jnp.dot(prolong_mat, linear, precision=PRECISE)
    for sweep in range(SMOOTH_FINE):
        solution = solution + FINE_WEIGHT * (rhs - apply_fine(solution)) / diag_fine
    return (jnp.take(solution, inverse, axis=1), jnp.take(coarse, inverse))


def solution(mesh):
    return jax.shard_map(
        local,
        mesh=mesh,
        in_specs=(
            P(None, ("mesh", "inner")),
            P(("mesh", "inner")),
            P(None, ("mesh", "inner")),
            P(None, ("mesh", "inner")),
            P(("mesh", "inner")),
            P(),
        ),
        out_specs=(P(None, ("mesh", "inner")), P(("mesh", "inner"))),
        check_vma=False,
    )
```

```python
import jax
import jax.numpy as jnp
import numpy as np
from jax import lax
from jax.sharding import PartitionSpec as P

SMOOTH_FINE = 3
SMOOTH_LIN = 2
BRICK_Y = 8

PENALTY = 2.0
FINE_WEIGHT = 0.6
LINEAR_WEIGHT = 0.5
PRECISE = lax.Precision.HIGHEST
AXES = ("mesh", "inner")


def shifted(value, axis, steps):
    count = lax.axis_size(axis)
    leading, last = (max(0, -steps), min(count, count - steps))
    return lax.ppermute(value, axis, [(source, source + steps) for source in range(leading, last)])


def main_diagonal(matrix):
    positions = np.arange(matrix.shape[0])
    return matrix[positions, positions]


def build_tables():
    line_stiff = np.array(
        [
            [1.0, -1.0, 0.0, 0.0],
            [-1.0, 2.0, -1.0, 0.0],
            [0.0, -1.0, 2.0, -1.0],
            [0.0, 0.0, -1.0, 1.0],
        ]
    )
    identity = np.eye(4)
    stiffness = (
        np.kron(np.kron(line_stiff, identity), identity)
        + np.kron(np.kron(identity, line_stiff), identity)
        + np.kron(np.kron(identity, identity), line_stiff)
    )
    ramp_basis = np.array([[1.0, 0.0], [2.0 / 3.0, 1.0 / 3.0], [1.0 / 3.0, 2.0 / 3.0], [0.0, 1.0]])
    prolong = np.kron(np.kron(ramp_basis, ramp_basis), ramp_basis)
    coarse_stiff = prolong.T @ stiffness @ prolong
    small_mass = ramp_basis.T @ ramp_basis
    face_mass = np.kron(small_mass, small_mass)
    return (stiffness, prolong, coarse_stiff, face_mass)


def face_slices(points):
    grid_ids = np.arange(points**3).reshape(points, points, points)
    last_index = points - 1
    return [
        grid_ids[0],
        grid_ids[last_index],
        grid_ids[:, 0],
        grid_ids[:, last_index],
        grid_ids[:, :, 0],
        grid_ids[:, :, last_index],
    ]


def lifting(points, face_mat):
    node_total = points**3
    per_face = points * points
    slices = face_slices(points)
    result = np.zeros((node_total, 6 * per_face))
    for face in range(6):
        select = np.zeros((node_total, per_face))
        select[slices[face].ravel(), np.arange(per_face)] = 1.0
        result[:, face * per_face : (face + 1) * per_face] = PENALTY * (select @ face_mat)
    return result


def face_diagonal(points, face_mat):
    result = np.zeros(points**3)
    for face_ids in face_slices(points):
        result[face_ids.ravel()] += PENALTY * main_diagonal(face_mat)
    return result


def stiff_and_traces(stiff, points):
    node_total = points**3
    per_face = points * points
    select = np.zeros((6 * per_face, node_total))
    for face, ids in enumerate(face_slices(points)):
        select[face * per_face + np.arange(per_face), ids.ravel()] = 1.0
    return np.concatenate([stiff, select], axis=0)


def shift_columns(values, offset):
    rows, width = values.shape
    pad = jnp.zeros((rows, abs(offset)), values.dtype)
    if offset > 0:
        return jnp.concatenate([values[:, offset:], pad], axis=1)
    return jnp.concatenate([pad, values[:, : width + offset]], axis=1)


def scale_of(level):
    return 96.0 * PENALTY * (8.0 * 2.0**level) ** (2.0 / 3.0)


def local(source, density, neighbours, halo_sends, aggregate, partner_map):
    stiffness, prolong, coarse_stiff, face_mass = build_tables()
    big_fine = jnp.asarray(stiff_and_traces(stiffness, 4), jnp.float32)
    big_lin = jnp.asarray(stiff_and_traces(coarse_stiff, 2), jnp.float32)
    prolong_mat = jnp.asarray(prolong, jnp.float32)
    lift_fine = jnp.asarray(lifting(4, np.eye(16)), jnp.float32)
    lift_lin = jnp.asarray(lifting(2, face_mass), jnp.float32)
    diag_fine_k = jnp.asarray(main_diagonal(stiffness), jnp.float32)
    diag_fine_f = jnp.asarray(face_diagonal(4, np.eye(16)), jnp.float32)
    diag_lin_k = jnp.asarray(main_diagonal(coarse_stiff), jnp.float32)
    diag_lin_f = jnp.asarray(face_diagonal(2, face_mass), jnp.float32)
    elements = source.shape[1]
    layer = halo_sends.shape[1]
    groups_width = elements // 8

    ordering = jnp.concatenate([halo_sends[0], halo_sends[1]])
    inverse = jnp.zeros((elements,), jnp.int32).at[ordering].set(
        jnp.arange(elements, dtype=jnp.int32)
    )
    rhs = jnp.take(source, ordering, axis=1)
    dens = jnp.take(density, ordering)
    agg = jnp.take(aggregate, ordering)

    column = np.arange(elements)
    pos_x = column % layer // BRICK_Y
    pos_y = column % BRICK_Y
    last_x = layer // BRICK_Y - 1
    masks = [
        jnp.asarray(pos_x > 0),
        jnp.asarray(pos_x < last_x),
        jnp.asarray(pos_y > 0),
        jnp.asarray(pos_y < BRICK_Y - 1),
    ]
    offsets = [-BRICK_Y, BRICK_Y, -1, 1]

    diag_fine = dens[None, :] * diag_fine_k[:, None] + diag_fine_f[:, None]
    diag_lin = dens[None, :] * diag_lin_k[:, None] + diag_lin_f[:, None]

    def apply(nodal_field, big, lift, node_total, per_face):
        stacked = jnp.dot(big, nodal_field, precision=PRECISE)
        stiff_part = stacked[:node_total]
        traces = [
            stacked[node_total + f * per_face : node_total + (f + 1) * per_face] for f in range(6)
        ]
        rim_low = shifted(traces[5][:, layer:], AXES, 1)
        rim_high = shifted(traces[4][:, :layer], AXES, -1)
        jumps = []
        for face in range(4):
            other = shift_columns(traces[face ^ 1], offsets[face])
            jumps.append(traces[face] - jnp.where(masks[face][None, :], other, 0.0))
        jumps.append(traces[4] - jnp.concatenate([rim_low, traces[5][:, :layer]], axis=1))
        jumps.append(traces[5] - jnp.concatenate([traces[4][:, layer:], rim_high], axis=1))
        jumps = jnp.concatenate(jumps, axis=0)
        return dens[None, :] * stiff_part + jnp.dot(lift, jumps, precision=PRECISE)

    def apply_fine(nodal_field):
        return apply(nodal_field, big_fine, lift_fine, 64, 16)

    def apply_lin(nodal_field):
        return apply(nodal_field, big_lin, lift_lin, 8, 4)

    solution = FINE_WEIGHT * rhs / diag_fine
    for sweep in range(SMOOTH_FINE - 1):
        solution = solution + FINE_WEIGHT * (rhs - apply_fine(solution)) / diag_fine
    resid_fine = rhs - apply_fine(solution)
    resid_lin = jnp.dot(prolong_mat.T, resid_fine, precision=PRECISE)
    linear = LINEAR_WEIGHT * resid_lin / diag_lin
    for sweep in range(SMOOTH_LIN - 1):
        linear = linear + LINEAR_WEIGHT * (resid_lin - apply_lin(linear)) / diag_lin
    left_lin = resid_lin - apply_lin(linear)
    resid_elem = jnp.sum(left_lin, axis=0)

    group_ids = jnp.arange(groups_width, dtype=jnp.int32)
    agg_hot = agg[:, None] == group_ids[None, :]
    own_sums = jnp.sum(jnp.where(agg_hot, resid_elem[:, None], 0.0), axis=0)

    flat_index = lax.axis_index("mesh") * lax.axis_size("inner") + lax.axis_index("inner")
    devices = lax.axis_size("mesh") * lax.axis_size("inner")
    current = own_sums
    descent = []
    level = 0
    while 2**level < devices:
        partner = lax.ppermute(current, AXES, [(i, i ^ (1 << level)) for i in range(devices)])
        below_term = current / scale_of(level)
        is_lower = (flat_index >> level) % 2 == 0
        paired = jnp.where(
            is_lower, jnp.concatenate([current, partner]), jnp.concatenate([partner, current])
        )
        level += 1
        row_index = flat_index // 2**level * 2**level + (2 ** (level - 1) - 1)
        parents = lax.dynamic_index_in_dim(partner_map, row_index, 0, keepdims=False)
        hot = parents[:, None] == group_ids[None, :]
        current = jnp.sum(jnp.where(hot, paired[:, None], 0.0), axis=0)
        descent.append((hot, is_lower, below_term))
    total = current / scale_of(level)
    for hot, is_lower, below_term in reversed(descent):
        children = jnp.sum(jnp.where(hot, total[None, :], 0.0), axis=1)
        total = (
            jnp.where(is_lower, children[:groups_width], children[groups_width:]) + below_term
        )
    own_total = total
    coarse = resid_elem / (96.0 * PENALTY) + jnp.sum(
        jnp.where(agg_hot, own_total[None, :], 0.0), axis=1
    )

    linear = linear + coarse[None, :]
    for sweep in range(SMOOTH_LIN):
        linear = linear + LINEAR_WEIGHT * (resid_lin - apply_lin(linear)) / diag_lin
    solution = solution + jnp.dot(prolong_mat, linear, precision=PRECISE)
    for sweep in range(SMOOTH_FINE):
        solution = solution + FINE_WEIGHT * (rhs - apply_fine(solution)) / diag_fine
    return (jnp.take(solution, inverse, axis=1), jnp.take(coarse, inverse))


def solution(mesh):
    return jax.shard_map(
        local,
        mesh=mesh,
        in_specs=(
            P(None, ("mesh", "inner")),
            P(("mesh", "inner")),
            P(None, ("mesh", "inner")),
            P(None, ("mesh", "inner")),
            P(("mesh", "inner")),
            P(),
        ),
        out_specs=(P(None, ("mesh", "inner")), P(("mesh", "inner"))),
        check_vma=False,
    )
```

```python
import jax
import jax.numpy as jnp
import numpy as np
from jax import lax
from jax.sharding import PartitionSpec as P

SMOOTH_FINE = 3
SMOOTH_LIN = 2
BRICK_Y = 8

PENALTY = 2.0
FINE_WEIGHT = 0.6
LINEAR_WEIGHT = 0.5
PRECISE = lax.Precision.HIGHEST
AXES = ("mesh", "inner")


def shifted(value, axis, steps):
    count = lax.axis_size(axis)
    leading, last = (max(0, -steps), min(count, count - steps))
    return lax.ppermute(value, axis, [(source, source + steps) for source in range(leading, last)])


def main_diagonal(matrix):
    positions = np.arange(matrix.shape[0])
    return matrix[positions, positions]


def build_tables():
    line_stiff = np.array(
        [
            [1.0, -1.0, 0.0, 0.0],
            [-1.0, 2.0, -1.0, 0.0],
            [0.0, -1.0, 2.0, -1.0],
            [0.0, 0.0, -1.0, 1.0],
        ]
    )
    identity = np.eye(4)
    stiffness = (
        np.kron(np.kron(line_stiff, identity), identity)
        + np.kron(np.kron(identity, line_stiff), identity)
        + np.kron(np.kron(identity, identity), line_stiff)
    )
    ramp_basis = np.array([[1.0, 0.0], [2.0 / 3.0, 1.0 / 3.0], [1.0 / 3.0, 2.0 / 3.0], [0.0, 1.0]])
    prolong = np.kron(np.kron(ramp_basis, ramp_basis), ramp_basis)
    coarse_stiff = prolong.T @ stiffness @ prolong
    small_mass = ramp_basis.T @ ramp_basis
    face_mass = np.kron(small_mass, small_mass)
    return (stiffness, prolong, coarse_stiff, face_mass)


def face_slices(points):
    grid_ids = np.arange(points**3).reshape(points, points, points)
    last_index = points - 1
    return [
        grid_ids[0],
        grid_ids[last_index],
        grid_ids[:, 0],
        grid_ids[:, last_index],
        grid_ids[:, :, 0],
        grid_ids[:, :, last_index],
    ]


def lifting(points, face_mat):
    node_total = points**3
    per_face = points * points
    slices = face_slices(points)
    result = np.zeros((node_total, 6 * per_face))
    for face in range(6):
        select = np.zeros((node_total, per_face))
        select[slices[face].ravel(), np.arange(per_face)] = 1.0
        result[:, face * per_face : (face + 1) * per_face] = PENALTY * (select @ face_mat)
    return result


def face_diagonal(points, face_mat):
    result = np.zeros(points**3)
    for face_ids in face_slices(points):
        result[face_ids.ravel()] += PENALTY * main_diagonal(face_mat)
    return result


def stiff_and_traces(stiff, points):
    node_total = points**3
    per_face = points * points
    select = np.zeros((6 * per_face, node_total))
    for face, ids in enumerate(face_slices(points)):
        select[face * per_face + np.arange(per_face), ids.ravel()] = 1.0
    return np.concatenate([stiff, select], axis=0)


def shift_columns(values, offset):
    rows, width = values.shape
    pad = jnp.zeros((rows, abs(offset)), values.dtype)
    if offset > 0:
        return jnp.concatenate([values[:, offset:], pad], axis=1)
    return jnp.concatenate([pad, values[:, : width + offset]], axis=1)


def snake_places(mesh_size, inner_size, y_size=4, cores=2):
    places = np.zeros(mesh_size * inner_size, np.int64)
    for slab in range(mesh_size * inner_size):
        row, inner = divmod(slab, inner_size)
        z, rest = divmod(row, y_size * cores)
        y, core = divmod(rest, cores)
        x_place = inner if core % 2 == 0 else inner_size - 1 - inner
        y_place = y if z % 2 == 0 else y_size - 1 - y
        places[slab] = ((z * y_size + y_place) * cores + core) * inner_size + x_place
    return places


def scale_of(level):
    return 96.0 * PENALTY * (8.0 * 2.0**level) ** (2.0 / 3.0)


def local(source, density, neighbours, halo_sends, aggregate, partner_map):
    stiffness, prolong, coarse_stiff, face_mass = build_tables()
    big_fine = jnp.asarray(stiff_and_traces(stiffness, 4), jnp.float32)
    big_lin = jnp.asarray(stiff_and_traces(coarse_stiff, 2), jnp.float32)
    prolong_mat = jnp.asarray(prolong, jnp.float32)
    lift_fine = jnp.asarray(lifting(4, np.eye(16)), jnp.float32)
    lift_lin = jnp.asarray(lifting(2, face_mass), jnp.float32)
    diag_fine_k = jnp.asarray(main_diagonal(stiffness), jnp.float32)
    diag_fine_f = jnp.asarray(face_diagonal(4, np.eye(16)), jnp.float32)
    diag_lin_k = jnp.asarray(main_diagonal(coarse_stiff), jnp.float32)
    diag_lin_f = jnp.asarray(face_diagonal(2, face_mass), jnp.float32)
    elements = source.shape[1]
    layer = halo_sends.shape[1]
    groups_width = elements // 8

    ordering = jnp.concatenate([halo_sends[0], halo_sends[1]])
    inverse = jnp.zeros((elements,), jnp.int32).at[ordering].set(
        jnp.arange(elements, dtype=jnp.int32)
    )
    rhs = jnp.take(source, ordering, axis=1)
    dens = jnp.take(density, ordering)
    agg = jnp.take(aggregate, ordering)

    devices = lax.axis_size("mesh") * lax.axis_size("inner")
    places = snake_places(lax.axis_size("mesh"), lax.axis_size("inner"))
    slab_of = np.argsort(places)
    here = lax.axis_index("mesh") * lax.axis_size("inner") + lax.axis_index("inner")
    flat_index = jnp.asarray(slab_of, jnp.int32)[here]
    bundle = jnp.concatenate([rhs, dens[None, :], agg.astype(jnp.float32)[None, :]], axis=0)
    bundle = lax.ppermute(bundle, AXES, [(q, int(places[q])) for q in range(devices)])
    rhs = bundle[:-2]
    dens = bundle[-2]
    agg = bundle[-1].astype(jnp.int32)
    up_pairs = [(int(places[d]), int(places[d + 1])) for d in range(devices - 1)]
    down_pairs = [(b, a) for a, b in up_pairs]

    column = np.arange(elements)
    pos_x = column % layer // BRICK_Y
    pos_y = column % BRICK_Y
    last_x = layer // BRICK_Y - 1
    masks = [
        jnp.asarray(pos_x > 0),
        jnp.asarray(pos_x < last_x),
        jnp.asarray(pos_y > 0),
        jnp.asarray(pos_y < BRICK_Y - 1),
    ]
    offsets = [-BRICK_Y, BRICK_Y, -1, 1]

    diag_fine = dens[None, :] * diag_fine_k[:, None] + diag_fine_f[:, None]
    diag_lin = dens[None, :] * diag_lin_k[:, None] + diag_lin_f[:, None]

    def apply(nodal_field, big, lift, node_total, per_face):
        stacked = jnp.dot(big, nodal_field, precision=PRECISE)
        stiff_part = stacked[:node_total]
        traces = [
            stacked[node_total + f * per_face : node_total + (f + 1) * per_face] for f in range(6)
        ]
        rim_low = lax.ppermute(traces[5][:, layer:], AXES, up_pairs)
        rim_high = lax.ppermute(traces[4][:, :layer], AXES, down_pairs)
        jumps = []
        for face in range(4):
            other = shift_columns(traces[face ^ 1], offsets[face])
            jumps.append(traces[face] - jnp.where(masks[face][None, :], other, 0.0))
        jumps.append(traces[4] - jnp.concatenate([rim_low, traces[5][:, :layer]], axis=1))
        jumps.append(traces[5] - jnp.concatenate([traces[4][:, layer:], rim_high], axis=1))
        jumps = jnp.concatenate(jumps, axis=0)
        return dens[None, :] * stiff_part + jnp.dot(lift, jumps, precision=PRECISE)

    def apply_fine(nodal_field):
        return apply(nodal_field, big_fine, lift_fine, 64, 16)

    def apply_lin(nodal_field):
        return apply(nodal_field, big_lin, lift_lin, 8, 4)

    solution = FINE_WEIGHT * rhs / diag_fine
    for sweep in range(SMOOTH_FINE - 1):
        solution = solution + FINE_WEIGHT * (rhs - apply_fine(solution)) / diag_fine
    resid_fine = rhs - apply_fine(solution)
    resid_lin = jnp.dot(prolong_mat.T, resid_fine, precision=PRECISE)
    linear = LINEAR_WEIGHT * resid_lin / diag_lin
    for sweep in range(SMOOTH_LIN - 1):
        linear = linear + LINEAR_WEIGHT * (resid_lin - apply_lin(linear)) / diag_lin
    left_lin = resid_lin - apply_lin(linear)
    resid_elem = jnp.sum(left_lin, axis=0)

    group_ids = jnp.arange(groups_width, dtype=jnp.int32)
    agg_hot = agg[:, None] == group_ids[None, :]
    own_sums = jnp.sum(jnp.where(agg_hot, resid_elem[:, None], 0.0), axis=0)

    current = own_sums
    descent = []
    level = 0
    while 2**level < devices:
        pairs = [(int(places[d]), int(places[d ^ (1 << level)])) for d in range(devices)]
        partner = lax.ppermute(current, AXES, pairs)
        below_term = current / scale_of(level)
        is_lower = (flat_index >> level) % 2 == 0
        paired = jnp.where(
            is_lower, jnp.concatenate([current, partner]), jnp.concatenate([partner, current])
        )
        level += 1
        row_index = flat_index // 2**level * 2**level + (2 ** (level - 1) - 1)
        parents = lax.dynamic_index_in_dim(partner_map, row_index, 0, keepdims=False)
        hot = parents[:, None] == group_ids[None, :]
        current = jnp.sum(jnp.where(hot, paired[:, None], 0.0), axis=0)
        descent.append((hot, is_lower, below_term))
    total = current / scale_of(level)
    for hot, is_lower, below_term in reversed(descent):
        children = jnp.sum(jnp.where(hot, total[None, :], 0.0), axis=1)
        total = (
            jnp.where(is_lower, children[:groups_width], children[groups_width:]) + below_term
        )
    own_total = total
    coarse = resid_elem / (96.0 * PENALTY) + jnp.sum(
        jnp.where(agg_hot, own_total[None, :], 0.0), axis=1
    )

    linear = linear + coarse[None, :]
    for sweep in range(SMOOTH_LIN):
        linear = linear + LINEAR_WEIGHT * (resid_lin - apply_lin(linear)) / diag_lin
    solution = solution + jnp.dot(prolong_mat, linear, precision=PRECISE)
    for sweep in range(SMOOTH_FINE):
        solution = solution + FINE_WEIGHT * (rhs - apply_fine(solution)) / diag_fine
    result = jnp.concatenate([solution, coarse[None, :]], axis=0)
    result = lax.ppermute(result, AXES, [(int(places[d]), d) for d in range(devices)])
    return (jnp.take(result[:-1], inverse, axis=1), jnp.take(result[-1], inverse))


def solution(mesh):
    return jax.shard_map(
        local,
        mesh=mesh,
        in_specs=(
            P(None, ("mesh", "inner")),
            P(("mesh", "inner")),
            P(None, ("mesh", "inner")),
            P(None, ("mesh", "inner")),
            P(("mesh", "inner")),
            P(),
        ),
        out_specs=(P(None, ("mesh", "inner")), P(("mesh", "inner"))),
        check_vma=False,
    )
```

```python
import jax
import jax.numpy as jnp
import numpy as np
from jax import lax
from jax.sharding import PartitionSpec as P

SMOOTH_FINE = 3
SMOOTH_LIN = 2
BRICK_Y = 8

PENALTY = 2.0
FINE_WEIGHT = 0.6
LINEAR_WEIGHT = 0.5
PRECISE = lax.Precision.HIGHEST
AXES = ("mesh", "inner")


def shifted(value, axis, steps):
    count = lax.axis_size(axis)
    leading, last = (max(0, -steps), min(count, count - steps))
    return lax.ppermute(value, axis, [(source, source + steps) for source in range(leading, last)])


def main_diagonal(matrix):
    positions = np.arange(matrix.shape[0])
    return matrix[positions, positions]


def build_tables():
    line_stiff = np.array(
        [
            [1.0, -1.0, 0.0, 0.0],
            [-1.0, 2.0, -1.0, 0.0],
            [0.0, -1.0, 2.0, -1.0],
            [0.0, 0.0, -1.0, 1.0],
        ]
    )
    identity = np.eye(4)
    stiffness = (
        np.kron(np.kron(line_stiff, identity), identity)
        + np.kron(np.kron(identity, line_stiff), identity)
        + np.kron(np.kron(identity, identity), line_stiff)
    )
    ramp_basis = np.array([[1.0, 0.0], [2.0 / 3.0, 1.0 / 3.0], [1.0 / 3.0, 2.0 / 3.0], [0.0, 1.0]])
    prolong = np.kron(np.kron(ramp_basis, ramp_basis), ramp_basis)
    coarse_stiff = prolong.T @ stiffness @ prolong
    small_mass = ramp_basis.T @ ramp_basis
    face_mass = np.kron(small_mass, small_mass)
    return (stiffness, prolong, coarse_stiff, face_mass)


def face_slices(points):
    grid_ids = np.arange(points**3).reshape(points, points, points)
    last_index = points - 1
    return [
        grid_ids[0],
        grid_ids[last_index],
        grid_ids[:, 0],
        grid_ids[:, last_index],
        grid_ids[:, :, 0],
        grid_ids[:, :, last_index],
    ]


def lifting(points, face_mat):
    node_total = points**3
    per_face = points * points
    slices = face_slices(points)
    result = np.zeros((node_total, 6 * per_face))
    for face in range(6):
        select = np.zeros((node_total, per_face))
        select[slices[face].ravel(), np.arange(per_face)] = 1.0
        result[:, face * per_face : (face + 1) * per_face] = PENALTY * (select @ face_mat)
    return result


def face_diagonal(points, face_mat):
    result = np.zeros(points**3)
    for face_ids in face_slices(points):
        result[face_ids.ravel()] += PENALTY * main_diagonal(face_mat)
    return result


def stiff_and_traces(stiff, points):
    node_total = points**3
    per_face = points * points
    select = np.zeros((6 * per_face, node_total))
    for face, ids in enumerate(face_slices(points)):
        select[face * per_face + np.arange(per_face), ids.ravel()] = 1.0
    return np.concatenate([stiff, select], axis=0)


def shift_columns(values, offset):
    rows, width = values.shape
    pad = jnp.zeros((rows, abs(offset)), values.dtype)
    if offset > 0:
        return jnp.concatenate([values[:, offset:], pad], axis=1)
    return jnp.concatenate([pad, values[:, : width + offset]], axis=1)


def snake_places(mesh_size, inner_size, y_size=4, cores=2):
    places = np.zeros(mesh_size * inner_size, np.int64)
    for slab in range(mesh_size * inner_size):
        row, inner = divmod(slab, inner_size)
        z, rest = divmod(row, y_size * cores)
        y, core = divmod(rest, cores)
        x_place = inner if core % 2 == 0 else inner_size - 1 - inner
        y_place = y if z % 2 == 0 else y_size - 1 - y
        places[slab] = ((z * y_size + y_place) * cores + core) * inner_size + x_place
    return places


def scale_of(level):
    return 96.0 * PENALTY * (8.0 * 2.0**level) ** (2.0 / 3.0)


def local(source, density, neighbours, halo_sends, aggregate, partner_map):
    stiffness, prolong, coarse_stiff, face_mass = build_tables()
    big_fine = jnp.asarray(stiff_and_traces(stiffness, 4), jnp.float32)
    big_lin = jnp.asarray(stiff_and_traces(coarse_stiff, 2), jnp.float32)
    prolong_mat = jnp.asarray(prolong, jnp.float32)
    lift_fine = jnp.asarray(lifting(4, np.eye(16)), jnp.float32)
    lift_lin = jnp.asarray(lifting(2, face_mass), jnp.float32)
    diag_fine_k = jnp.asarray(main_diagonal(stiffness), jnp.float32)
    diag_fine_f = jnp.asarray(face_diagonal(4, np.eye(16)), jnp.float32)
    diag_lin_k = jnp.asarray(main_diagonal(coarse_stiff), jnp.float32)
    diag_lin_f = jnp.asarray(face_diagonal(2, face_mass), jnp.float32)
    elements = source.shape[1]
    layer = halo_sends.shape[1]
    groups_width = elements // 8

    ordering = jnp.concatenate([halo_sends[0], halo_sends[1]])
    inverse = jnp.zeros((elements,), jnp.int32).at[ordering].set(
        jnp.arange(elements, dtype=jnp.int32)
    )
    rhs = jnp.take(source, ordering, axis=1)
    dens = jnp.take(density, ordering)
    agg = jnp.take(aggregate, ordering)

    devices = lax.axis_size("mesh") * lax.axis_size("inner")
    places = snake_places(lax.axis_size("mesh"), lax.axis_size("inner"))
    slab_of = np.argsort(places)
    here = lax.axis_index("mesh") * lax.axis_size("inner") + lax.axis_index("inner")
    flat_index = jnp.asarray(slab_of, jnp.int32)[here]
    bundle = jnp.concatenate([rhs, dens[None, :], agg.astype(jnp.float32)[None, :]], axis=0)
    bundle = lax.ppermute(bundle, AXES, [(q, int(places[q])) for q in range(devices)])
    rhs = bundle[:-2]
    dens = bundle[-2]
    agg = bundle[-1].astype(jnp.int32)
    first_pairs = []
    second_pairs = []
    for d in range(devices - 1):
        pairs = first_pairs if d % 2 == 0 else second_pairs
        pairs += [(int(places[d]), int(places[d + 1])), (int(places[d + 1]), int(places[d]))]
    is_even = flat_index % 2 == 0

    column = np.arange(elements)
    pos_x = column % layer // BRICK_Y
    pos_y = column % BRICK_Y
    last_x = layer // BRICK_Y - 1
    masks = [
        jnp.asarray(pos_x > 0),
        jnp.asarray(pos_x < last_x),
        jnp.asarray(pos_y > 0),
        jnp.asarray(pos_y < BRICK_Y - 1),
    ]
    offsets = [-BRICK_Y, BRICK_Y, -1, 1]

    diag_fine = dens[None, :] * diag_fine_k[:, None] + diag_fine_f[:, None]
    diag_lin = dens[None, :] * diag_lin_k[:, None] + diag_lin_f[:, None]

    def apply(nodal_field, big, lift, node_total, per_face):
        stacked = jnp.dot(big, nodal_field, precision=PRECISE)
        stiff_part = stacked[:node_total]
        traces = [
            stacked[node_total + f * per_face : node_total + (f + 1) * per_face] for f in range(6)
        ]
        send_up = traces[5][:, layer:]
        send_down = traces[4][:, :layer]
        first = lax.ppermute(jnp.where(is_even, send_up, send_down), AXES, first_pairs)
        second = lax.ppermute(jnp.where(is_even, send_down, send_up), AXES, second_pairs)
        rim_low = jnp.where(is_even, second, first)
        rim_high = jnp.where(is_even, first, second)
        jumps = []
        for face in range(4):
            other = shift_columns(traces[face ^ 1], offsets[face])
            jumps.append(traces[face] - jnp.where(masks[face][None, :], other, 0.0))
        jumps.append(traces[4] - jnp.concatenate([rim_low, traces[5][:, :layer]], axis=1))
        jumps.append(traces[5] - jnp.concatenate([traces[4][:, layer:], rim_high], axis=1))
        jumps = jnp.concatenate(jumps, axis=0)
        return dens[None, :] * stiff_part + jnp.dot(lift, jumps, precision=PRECISE)

    def apply_fine(nodal_field):
        return apply(nodal_field, big_fine, lift_fine, 64, 16)

    def apply_lin(nodal_field):
        return apply(nodal_field, big_lin, lift_lin, 8, 4)

    solution = FINE_WEIGHT * rhs / diag_fine
    for sweep in range(SMOOTH_FINE - 1):
        solution = solution + FINE_WEIGHT * (rhs - apply_fine(solution)) / diag_fine
    resid_fine = rhs - apply_fine(solution)
    resid_lin = jnp.dot(prolong_mat.T, resid_fine, precision=PRECISE)
    linear = LINEAR_WEIGHT * resid_lin / diag_lin
    for sweep in range(SMOOTH_LIN - 1):
        linear = linear + LINEAR_WEIGHT * (resid_lin - apply_lin(linear)) / diag_lin
    left_lin = resid_lin - apply_lin(linear)
    resid_elem = jnp.sum(left_lin, axis=0)

    group_ids = jnp.arange(groups_width, dtype=jnp.int32)
    agg_hot = agg[:, None] == group_ids[None, :]
    own_sums = jnp.sum(jnp.where(agg_hot, resid_elem[:, None], 0.0), axis=0)

    current = own_sums
    descent = []
    level = 0
    while 2**level < devices:
        pairs = [(int(places[d]), int(places[d ^ (1 << level)])) for d in range(devices)]
        partner = lax.ppermute(current, AXES, pairs)
        below_term = current / scale_of(level)
        is_lower = (flat_index >> level) % 2 == 0
        paired = jnp.where(
            is_lower, jnp.concatenate([current, partner]), jnp.concatenate([partner, current])
        )
        level += 1
        row_index = flat_index // 2**level * 2**level + (2 ** (level - 1) - 1)
        parents = lax.dynamic_index_in_dim(partner_map, row_index, 0, keepdims=False)
        hot = parents[:, None] == group_ids[None, :]
        current = jnp.sum(jnp.where(hot, paired[:, None], 0.0), axis=0)
        descent.append((hot, is_lower, below_term))
    total = current / scale_of(level)
    for hot, is_lower, below_term in reversed(descent):
        children = jnp.sum(jnp.where(hot, total[None, :], 0.0), axis=1)
        total = (
            jnp.where(is_lower, children[:groups_width], children[groups_width:]) + below_term
        )
    own_total = total
    coarse = resid_elem / (96.0 * PENALTY) + jnp.sum(
        jnp.where(agg_hot, own_total[None, :], 0.0), axis=1
    )

    linear = linear + coarse[None, :]
    for sweep in range(SMOOTH_LIN):
        linear = linear + LINEAR_WEIGHT * (resid_lin - apply_lin(linear)) / diag_lin
    solution = solution + jnp.dot(prolong_mat, linear, precision=PRECISE)
    for sweep in range(SMOOTH_FINE):
        solution = solution + FINE_WEIGHT * (rhs - apply_fine(solution)) / diag_fine
    result = jnp.concatenate([solution, coarse[None, :]], axis=0)
    result = lax.ppermute(result, AXES, [(int(places[d]), d) for d in range(devices)])
    return (jnp.take(result[:-1], inverse, axis=1), jnp.take(result[-1], inverse))


def solution(mesh):
    return jax.shard_map(
        local,
        mesh=mesh,
        in_specs=(
            P(None, ("mesh", "inner")),
            P(("mesh", "inner")),
            P(None, ("mesh", "inner")),
            P(None, ("mesh", "inner")),
            P(("mesh", "inner")),
            P(),
        ),
        out_specs=(P(None, ("mesh", "inner")), P(("mesh", "inner"))),
        check_vma=False,
    )
```

```python
import jax
import jax.numpy as jnp
import numpy as np
from jax import lax
from jax.sharding import PartitionSpec as P

SMOOTH_FINE = 3
SMOOTH_LIN = 2
BRICK_Y = 8

PENALTY = 2.0
FINE_WEIGHT = 0.6
LINEAR_WEIGHT = 0.5
PRECISE = lax.Precision.HIGHEST
AXES = ("mesh", "inner")


def shifted(value, axis, steps):
    count = lax.axis_size(axis)
    leading, last = (max(0, -steps), min(count, count - steps))
    return lax.ppermute(value, axis, [(source, source + steps) for source in range(leading, last)])


def main_diagonal(matrix):
    positions = np.arange(matrix.shape[0])
    return matrix[positions, positions]


def build_tables():
    line_stiff = np.array(
        [
            [1.0, -1.0, 0.0, 0.0],
            [-1.0, 2.0, -1.0, 0.0],
            [0.0, -1.0, 2.0, -1.0],
            [0.0, 0.0, -1.0, 1.0],
        ]
    )
    identity = np.eye(4)
    stiffness = (
        np.kron(np.kron(line_stiff, identity), identity)
        + np.kron(np.kron(identity, line_stiff), identity)
        + np.kron(np.kron(identity, identity), line_stiff)
    )
    ramp_basis = np.array([[1.0, 0.0], [2.0 / 3.0, 1.0 / 3.0], [1.0 / 3.0, 2.0 / 3.0], [0.0, 1.0]])
    prolong = np.kron(np.kron(ramp_basis, ramp_basis), ramp_basis)
    coarse_stiff = prolong.T @ stiffness @ prolong
    small_mass = ramp_basis.T @ ramp_basis
    face_mass = np.kron(small_mass, small_mass)
    return (stiffness, prolong, coarse_stiff, face_mass)


def face_slices(points):
    grid_ids = np.arange(points**3).reshape(points, points, points)
    last_index = points - 1
    return [
        grid_ids[0],
        grid_ids[last_index],
        grid_ids[:, 0],
        grid_ids[:, last_index],
        grid_ids[:, :, 0],
        grid_ids[:, :, last_index],
    ]


def lifting(points, face_mat):
    node_total = points**3
    per_face = points * points
    slices = face_slices(points)
    result = np.zeros((node_total, 6 * per_face))
    for face in range(6):
        select = np.zeros((node_total, per_face))
        select[slices[face].ravel(), np.arange(per_face)] = 1.0
        result[:, face * per_face : (face + 1) * per_face] = PENALTY * (select @ face_mat)
    return result


def face_diagonal(points, face_mat):
    result = np.zeros(points**3)
    for face_ids in face_slices(points):
        result[face_ids.ravel()] += PENALTY * main_diagonal(face_mat)
    return result


def stiff_and_traces(stiff, points):
    node_total = points**3
    per_face = points * points
    select = np.zeros((6 * per_face, node_total))
    for face, ids in enumerate(face_slices(points)):
        select[face * per_face + np.arange(per_face), ids.ravel()] = 1.0
    return np.concatenate([stiff, select], axis=0)


def shift_columns(values, offset):
    rows, width = values.shape
    pad = jnp.zeros((rows, abs(offset)), values.dtype)
    if offset > 0:
        return jnp.concatenate([values[:, offset:], pad], axis=1)
    return jnp.concatenate([pad, values[:, : width + offset]], axis=1)


def snake_places(mesh_size, inner_size, y_size=4, cores=2):
    places = np.zeros(mesh_size * inner_size, np.int64)
    for slab in range(mesh_size * inner_size):
        row, inner = divmod(slab, inner_size)
        z, rest = divmod(row, y_size * cores)
        y, core = divmod(rest, cores)
        x_place = inner if core % 2 == 0 else inner_size - 1 - inner
        y_place = y if z % 2 == 0 else y_size - 1 - y
        places[slab] = ((z * y_size + y_place) * cores + core) * inner_size + x_place
    return places


def scale_of(level):
    return 96.0 * PENALTY * (8.0 * 2.0**level) ** (2.0 / 3.0)


def local(source, density, neighbours, halo_sends, aggregate, partner_map):
    stiffness, prolong, coarse_stiff, face_mass = build_tables()
    big_fine = jnp.asarray(stiff_and_traces(stiffness, 4), jnp.float32)
    big_lin = jnp.asarray(stiff_and_traces(coarse_stiff, 2), jnp.float32)
    prolong_mat = jnp.asarray(prolong, jnp.float32)
    lift_fine = jnp.asarray(lifting(4, np.eye(16)), jnp.float32)
    lift_lin = jnp.asarray(lifting(2, face_mass), jnp.float32)
    diag_fine_k = jnp.asarray(main_diagonal(stiffness), jnp.float32)
    diag_fine_f = jnp.asarray(face_diagonal(4, np.eye(16)), jnp.float32)
    diag_lin_k = jnp.asarray(main_diagonal(coarse_stiff), jnp.float32)
    diag_lin_f = jnp.asarray(face_diagonal(2, face_mass), jnp.float32)
    elements = source.shape[1]
    layer = halo_sends.shape[1]
    groups_width = elements // 8

    ordering = jnp.concatenate([halo_sends[0], halo_sends[1]])
    to_brick = (
        jnp.arange(elements, dtype=jnp.int32)[:, None] == ordering[None, :]
    ).astype(jnp.float32)
    stacked_inputs = jnp.concatenate(
        [source, density[None, :], aggregate.astype(jnp.float32)[None, :]], axis=0
    )
    bundle = jnp.dot(stacked_inputs, to_brick, precision=PRECISE)

    devices = lax.axis_size("mesh") * lax.axis_size("inner")
    places = snake_places(lax.axis_size("mesh"), lax.axis_size("inner"))
    slab_of = np.argsort(places)
    here = lax.axis_index("mesh") * lax.axis_size("inner") + lax.axis_index("inner")
    flat_index = jnp.asarray(slab_of, jnp.int32)[here]
    bundle = lax.ppermute(bundle, AXES, [(q, int(places[q])) for q in range(devices)])
    rhs = bundle[:-2]
    dens = bundle[-2]
    agg = jnp.round(bundle[-1]).astype(jnp.int32)
    up_pairs = [(int(places[d]), int(places[d + 1])) for d in range(devices - 1)]
    down_pairs = [(b, a) for a, b in up_pairs]

    column = np.arange(elements)
    pos_x = column % layer // BRICK_Y
    pos_y = column % BRICK_Y
    last_x = layer // BRICK_Y - 1
    masks = [
        jnp.asarray(pos_x > 0),
        jnp.asarray(pos_x < last_x),
        jnp.asarray(pos_y > 0),
        jnp.asarray(pos_y < BRICK_Y - 1),
    ]
    offsets = [-BRICK_Y, BRICK_Y, -1, 1]

    diag_fine = dens[None, :] * diag_fine_k[:, None] + diag_fine_f[:, None]
    diag_lin = dens[None, :] * diag_lin_k[:, None] + diag_lin_f[:, None]

    def apply(nodal_field, big, lift, node_total, per_face):
        stacked = jnp.dot(big, nodal_field, precision=PRECISE)
        stiff_part = stacked[:node_total]
        traces = [
            stacked[node_total + f * per_face : node_total + (f + 1) * per_face] for f in range(6)
        ]
        rim_low = lax.ppermute(traces[5][:, layer:], AXES, up_pairs)
        rim_high = lax.ppermute(traces[4][:, :layer], AXES, down_pairs)
        jumps = []
        for face in range(4):
            other = shift_columns(traces[face ^ 1], offsets[face])
            jumps.append(traces[face] - jnp.where(masks[face][None, :], other, 0.0))
        jumps.append(traces[4] - jnp.concatenate([rim_low, traces[5][:, :layer]], axis=1))
        jumps.append(traces[5] - jnp.concatenate([traces[4][:, layer:], rim_high], axis=1))
        jumps = jnp.concatenate(jumps, axis=0)
        return dens[None, :] * stiff_part + jnp.dot(lift, jumps, precision=PRECISE)

    def apply_fine(nodal_field):
        return apply(nodal_field, big_fine, lift_fine, 64, 16)

    def apply_lin(nodal_field):
        return apply(nodal_field, big_lin, lift_lin, 8, 4)

    solution = FINE_WEIGHT * rhs / diag_fine
    for sweep in range(SMOOTH_FINE - 1):
        solution = solution + FINE_WEIGHT * (rhs - apply_fine(solution)) / diag_fine
    resid_fine = rhs - apply_fine(solution)
    resid_lin = jnp.dot(prolong_mat.T, resid_fine, precision=PRECISE)
    linear = LINEAR_WEIGHT * resid_lin / diag_lin
    for sweep in range(SMOOTH_LIN - 1):
        linear = linear + LINEAR_WEIGHT * (resid_lin - apply_lin(linear)) / diag_lin
    left_lin = resid_lin - apply_lin(linear)
    resid_elem = jnp.sum(left_lin, axis=0)

    group_ids = jnp.arange(groups_width, dtype=jnp.int32)
    agg_hot = agg[:, None] == group_ids[None, :]
    own_sums = jnp.sum(jnp.where(agg_hot, resid_elem[:, None], 0.0), axis=0)

    current = own_sums
    descent = []
    level = 0
    while 2**level < devices:
        pairs = [(int(places[d]), int(places[d ^ (1 << level)])) for d in range(devices)]
        partner = lax.ppermute(current, AXES, pairs)
        below_term = current / scale_of(level)
        is_lower = (flat_index >> level) % 2 == 0
        paired = jnp.where(
            is_lower, jnp.concatenate([current, partner]), jnp.concatenate([partner, current])
        )
        level += 1
        row_index = flat_index // 2**level * 2**level + (2 ** (level - 1) - 1)
        parents = lax.dynamic_index_in_dim(partner_map, row_index, 0, keepdims=False)
        hot = parents[:, None] == group_ids[None, :]
        current = jnp.sum(jnp.where(hot, paired[:, None], 0.0), axis=0)
        descent.append((hot, is_lower, below_term))
    total = current / scale_of(level)
    for hot, is_lower, below_term in reversed(descent):
        children = jnp.sum(jnp.where(hot, total[None, :], 0.0), axis=1)
        total = (
            jnp.where(is_lower, children[:groups_width], children[groups_width:]) + below_term
        )
    own_total = total
    coarse = resid_elem / (96.0 * PENALTY) + jnp.sum(
        jnp.where(agg_hot, own_total[None, :], 0.0), axis=1
    )

    linear = linear + coarse[None, :]
    for sweep in range(SMOOTH_LIN):
        linear = linear + LINEAR_WEIGHT * (resid_lin - apply_lin(linear)) / diag_lin
    solution = solution + jnp.dot(prolong_mat, linear, precision=PRECISE)
    for sweep in range(SMOOTH_FINE):
        solution = solution + FINE_WEIGHT * (rhs - apply_fine(solution)) / diag_fine
    result = jnp.concatenate([solution, coarse[None, :]], axis=0)
    result = lax.ppermute(result, AXES, [(int(places[d]), d) for d in range(devices)])
    result = lax.dot_general(
        result, to_brick, (((1,), (1,)), ((), ())), precision=PRECISE
    )
    return (result[:-1], result[-1])


def solution(mesh):
    return jax.shard_map(
        local,
        mesh=mesh,
        in_specs=(
            P(None, ("mesh", "inner")),
            P(("mesh", "inner")),
            P(None, ("mesh", "inner")),
            P(None, ("mesh", "inner")),
            P(("mesh", "inner")),
            P(),
        ),
        out_specs=(P(None, ("mesh", "inner")), P(("mesh", "inner"))),
        check_vma=False,
    )
```

```python
import jax
import jax.numpy as jnp
import numpy as np
from jax import lax
from jax.sharding import PartitionSpec as P

SMOOTH_FINE = 3
SMOOTH_LIN = 2
BRICK_Y = 8

PENALTY = 2.0
FINE_WEIGHT = 0.6
LINEAR_WEIGHT = 0.5
PRECISE = lax.Precision.HIGHEST
AXES = ("mesh", "inner")


def shifted(value, axis, steps):
    count = lax.axis_size(axis)
    leading, last = (max(0, -steps), min(count, count - steps))
    return lax.ppermute(value, axis, [(source, source + steps) for source in range(leading, last)])


def main_diagonal(matrix):
    positions = np.arange(matrix.shape[0])
    return matrix[positions, positions]


def build_tables():
    line_stiff = np.array(
        [
            [1.0, -1.0, 0.0, 0.0],
            [-1.0, 2.0, -1.0, 0.0],
            [0.0, -1.0, 2.0, -1.0],
            [0.0, 0.0, -1.0, 1.0],
        ]
    )
    identity = np.eye(4)
    stiffness = (
        np.kron(np.kron(line_stiff, identity), identity)
        + np.kron(np.kron(identity, line_stiff), identity)
        + np.kron(np.kron(identity, identity), line_stiff)
    )
    ramp_basis = np.array([[1.0, 0.0], [2.0 / 3.0, 1.0 / 3.0], [1.0 / 3.0, 2.0 / 3.0], [0.0, 1.0]])
    prolong = np.kron(np.kron(ramp_basis, ramp_basis), ramp_basis)
    coarse_stiff = prolong.T @ stiffness @ prolong
    small_mass = ramp_basis.T @ ramp_basis
    face_mass = np.kron(small_mass, small_mass)
    return (stiffness, prolong, coarse_stiff, face_mass)


def face_slices(points):
    grid_ids = np.arange(points**3).reshape(points, points, points)
    last_index = points - 1
    return [
        grid_ids[0],
        grid_ids[last_index],
        grid_ids[:, 0],
        grid_ids[:, last_index],
        grid_ids[:, :, 0],
        grid_ids[:, :, last_index],
    ]


def lifting(points, face_mat):
    node_total = points**3
    per_face = points * points
    slices = face_slices(points)
    result = np.zeros((node_total, 6 * per_face))
    for face in range(6):
        select = np.zeros((node_total, per_face))
        select[slices[face].ravel(), np.arange(per_face)] = 1.0
        result[:, face * per_face : (face + 1) * per_face] = PENALTY * (select @ face_mat)
    return result


def face_diagonal(points, face_mat):
    result = np.zeros(points**3)
    for face_ids in face_slices(points):
        result[face_ids.ravel()] += PENALTY * main_diagonal(face_mat)
    return result


def stiff_and_traces(stiff, points):
    node_total = points**3
    per_face = points * points
    select = np.zeros((6 * per_face, node_total))
    for face, ids in enumerate(face_slices(points)):
        select[face * per_face + np.arange(per_face), ids.ravel()] = 1.0
    return np.concatenate([stiff, select], axis=0)


def shift_columns(values, offset):
    rows, width = values.shape
    pad = jnp.zeros((rows, abs(offset)), values.dtype)
    if offset > 0:
        return jnp.concatenate([values[:, offset:], pad], axis=1)
    return jnp.concatenate([pad, values[:, : width + offset]], axis=1)


def snake_places(mesh_size, inner_size, y_size=4, cores=2):
    places = np.zeros(mesh_size * inner_size, np.int64)
    for slab in range(mesh_size * inner_size):
        row, inner = divmod(slab, inner_size)
        z, rest = divmod(row, y_size * cores)
        y, core = divmod(rest, cores)
        x_place = inner if core % 2 == 0 else inner_size - 1 - inner
        y_place = y if z % 2 == 0 else y_size - 1 - y
        places[slab] = ((z * y_size + y_place) * cores + core) * inner_size + x_place
    return places


def scale_of(level):
    return 96.0 * PENALTY * (8.0 * 2.0**level) ** (2.0 / 3.0)


def local(source, density, neighbours, halo_sends, aggregate, partner_map):
    stiffness, prolong, coarse_stiff, face_mass = build_tables()
    big_fine = jnp.asarray(stiff_and_traces(stiffness, 4), jnp.float32)
    big_lin = jnp.asarray(stiff_and_traces(coarse_stiff, 2), jnp.float32)
    prolong_mat = jnp.asarray(prolong, jnp.float32)
    lift_fine = jnp.asarray(lifting(4, np.eye(16)), jnp.float32)
    lift_lin = jnp.asarray(lifting(2, face_mass), jnp.float32)
    diag_fine_k = jnp.asarray(main_diagonal(stiffness), jnp.float32)
    diag_fine_f = jnp.asarray(face_diagonal(4, np.eye(16)), jnp.float32)
    diag_lin_k = jnp.asarray(main_diagonal(coarse_stiff), jnp.float32)
    diag_lin_f = jnp.asarray(face_diagonal(2, face_mass), jnp.float32)
    elements = source.shape[1]
    layer = halo_sends.shape[1]
    groups_width = elements // 8

    ordering = jnp.concatenate([halo_sends[0], halo_sends[1]])
    to_brick = (
        jnp.arange(elements, dtype=jnp.int32)[:, None] == ordering[None, :]
    ).astype(jnp.float32)
    stacked_inputs = jnp.concatenate(
        [source, density[None, :], aggregate.astype(jnp.float32)[None, :]], axis=0
    )
    bundle = jnp.dot(stacked_inputs, to_brick, precision=PRECISE)

    devices = lax.axis_size("mesh") * lax.axis_size("inner")
    places = snake_places(lax.axis_size("mesh"), lax.axis_size("inner"))
    slab_of = np.argsort(places)
    here = lax.axis_index("mesh") * lax.axis_size("inner") + lax.axis_index("inner")
    flat_index = jnp.asarray(slab_of, jnp.int32)[here]
    bundle = lax.ppermute(bundle, AXES, [(q, int(places[q])) for q in range(devices)])
    rhs = bundle[:-2]
    dens = bundle[-2]
    agg = jnp.round(bundle[-1]).astype(jnp.int32)
    up_pairs = [(int(places[d]), int(places[d + 1])) for d in range(devices - 1)]
    down_pairs = [(b, a) for a, b in up_pairs]

    column = np.arange(elements)
    pos_x = column % layer // BRICK_Y
    pos_y = column % BRICK_Y
    last_x = layer // BRICK_Y - 1
    masks = [
        jnp.asarray(pos_x > 0),
        jnp.asarray(pos_x < last_x),
        jnp.asarray(pos_y > 0),
        jnp.asarray(pos_y < BRICK_Y - 1),
    ]
    offsets = [-BRICK_Y, BRICK_Y, -1, 1]

    diag_fine = dens[None, :] * diag_fine_k[:, None] + diag_fine_f[:, None]
    diag_lin = dens[None, :] * diag_lin_k[:, None] + diag_lin_f[:, None]

    def apply(nodal_field, big, lift, node_total, per_face):
        stacked = jnp.dot(big, nodal_field, precision=PRECISE)
        stiff_part = stacked[:node_total]
        traces = [
            stacked[node_total + f * per_face : node_total + (f + 1) * per_face] for f in range(6)
        ]
        rim_low = lax.ppermute(traces[5][:, layer:], AXES, up_pairs)
        rim_high = lax.ppermute(traces[4][:, :layer], AXES, down_pairs)
        jumps = []
        for face in range(4):
            other = shift_columns(traces[face ^ 1], offsets[face])
            jumps.append(traces[face] - jnp.where(masks[face][None, :], other, 0.0))
        jumps.append(traces[4] - jnp.concatenate([rim_low, traces[5][:, :layer]], axis=1))
        jumps.append(traces[5] - jnp.concatenate([traces[4][:, layer:], rim_high], axis=1))
        jumps = jnp.concatenate(jumps, axis=0)
        return dens[None, :] * stiff_part + jnp.dot(lift, jumps, precision=PRECISE)

    wide_column = np.arange(3 * elements)
    wide_x = wide_column % layer // BRICK_Y
    wide_y = wide_column % BRICK_Y
    wide_masks = [
        jnp.asarray(wide_x > 0),
        jnp.asarray(wide_x < last_x),
        jnp.asarray(wide_y > 0),
        jnp.asarray(wide_y < BRICK_Y - 1),
    ]

    def apply_wide(nodal_field, wide_dens):
        stacked = jnp.dot(big_lin, nodal_field, precision=PRECISE)
        stiff_part = stacked[:8]
        traces = [stacked[8 + f * 4 : 8 + (f + 1) * 4] for f in range(6)]
        jumps = []
        for face in range(4):
            other = shift_columns(traces[face ^ 1], offsets[face])
            jumps.append(traces[face] - jnp.where(wide_masks[face][None, :], other, 0.0))
        jumps.append(traces[4] - shift_columns(traces[5], -layer))
        jumps.append(traces[5] - shift_columns(traces[4], layer))
        jumps = jnp.concatenate(jumps, axis=0)
        return wide_dens[None, :] * stiff_part + jnp.dot(lift_lin, jumps, precision=PRECISE)

    def apply_fine(nodal_field):
        return apply(nodal_field, big_fine, lift_fine, 64, 16)

    def apply_lin(nodal_field):
        return apply(nodal_field, big_lin, lift_lin, 8, 4)

    solution = FINE_WEIGHT * rhs / diag_fine
    for sweep in range(SMOOTH_FINE - 1):
        solution = solution + FINE_WEIGHT * (rhs - apply_fine(solution)) / diag_fine
    resid_fine = rhs - apply_fine(solution)
    resid_lin = jnp.dot(prolong_mat.T, resid_fine, precision=PRECISE)
    assert SMOOTH_LIN <= 2
    own = slice(elements, 2 * elements)
    slab = jnp.concatenate([resid_lin, dens[None, :]], axis=0)
    below = lax.ppermute(slab, AXES, up_pairs)
    above = lax.ppermute(slab, AXES, down_pairs)
    wide_resid = jnp.concatenate([below[:-1], resid_lin, above[:-1]], axis=1)
    wide_dens = jnp.concatenate([below[-1], dens, above[-1]])
    wide_diag = wide_dens[None, :] * diag_lin_k[:, None] + diag_lin_f[:, None]
    keep = jnp.concatenate(
        [
            jnp.full((elements,), flat_index > 0),
            jnp.ones((elements,), bool),
            jnp.full((elements,), flat_index < devices - 1),
        ]
    )[None, :]
    wide = LINEAR_WEIGHT * wide_resid / wide_diag
    for sweep in range(SMOOTH_LIN - 1):
        wide = wide + LINEAR_WEIGHT * (wide_resid - apply_wide(wide, wide_dens)) / wide_diag
        wide = jnp.where(keep, wide, 0.0)
    left_lin = resid_lin - apply_wide(wide, wide_dens)[:, own]
    linear = wide[:, own]
    resid_elem = jnp.sum(left_lin, axis=0)

    group_ids = jnp.arange(groups_width, dtype=jnp.int32)
    agg_hot = agg[:, None] == group_ids[None, :]
    own_sums = jnp.sum(jnp.where(agg_hot, resid_elem[:, None], 0.0), axis=0)

    current = own_sums
    descent = []
    level = 0
    while 2**level < devices:
        pairs = [(int(places[d]), int(places[d ^ (1 << level)])) for d in range(devices)]
        partner = lax.ppermute(current, AXES, pairs)
        below_term = current / scale_of(level)
        is_lower = (flat_index >> level) % 2 == 0
        paired = jnp.where(
            is_lower, jnp.concatenate([current, partner]), jnp.concatenate([partner, current])
        )
        level += 1
        row_index = flat_index // 2**level * 2**level + (2 ** (level - 1) - 1)
        parents = lax.dynamic_index_in_dim(partner_map, row_index, 0, keepdims=False)
        hot = parents[:, None] == group_ids[None, :]
        current = jnp.sum(jnp.where(hot, paired[:, None], 0.0), axis=0)
        descent.append((hot, is_lower, below_term))
    total = current / scale_of(level)
    for hot, is_lower, below_term in reversed(descent):
        children = jnp.sum(jnp.where(hot, total[None, :], 0.0), axis=1)
        total = (
            jnp.where(is_lower, children[:groups_width], children[groups_width:]) + below_term
        )
    own_total = total
    coarse = resid_elem / (96.0 * PENALTY) + jnp.sum(
        jnp.where(agg_hot, own_total[None, :], 0.0), axis=1
    )

    linear = linear + coarse[None, :]
    wide = jnp.concatenate(
        [
            lax.ppermute(linear, AXES, up_pairs),
            linear,
            lax.ppermute(linear, AXES, down_pairs),
        ],
        axis=1,
    )
    for sweep in range(SMOOTH_LIN):
        wide = wide + LINEAR_WEIGHT * (wide_resid - apply_wide(wide, wide_dens)) / wide_diag
        wide = jnp.where(keep, wide, 0.0)
    linear = wide[:, own]
    solution = solution + jnp.dot(prolong_mat, linear, precision=PRECISE)
    for sweep in range(SMOOTH_FINE):
        solution = solution + FINE_WEIGHT * (rhs - apply_fine(solution)) / diag_fine
    result = jnp.concatenate([solution, coarse[None, :]], axis=0)
    result = lax.ppermute(result, AXES, [(int(places[d]), d) for d in range(devices)])
    result = lax.dot_general(
        result, to_brick, (((1,), (1,)), ((), ())), precision=PRECISE
    )
    return (result[:-1], result[-1])


def solution(mesh):
    return jax.shard_map(
        local,
        mesh=mesh,
        in_specs=(
            P(None, ("mesh", "inner")),
            P(("mesh", "inner")),
            P(None, ("mesh", "inner")),
            P(None, ("mesh", "inner")),
            P(("mesh", "inner")),
            P(),
        ),
        out_specs=(P(None, ("mesh", "inner")), P(("mesh", "inner"))),
        check_vma=False,
    )
```

```python
import jax
import jax.numpy as jnp
import numpy as np
from jax import lax
from jax.sharding import PartitionSpec as P

SMOOTH_FINE = 3
SMOOTH_LIN = 2
BRICK_Y = 8

PENALTY = 2.0
FINE_WEIGHT = 0.6
LINEAR_WEIGHT = 0.5
PRECISE = lax.Precision.HIGHEST
AXES = ("mesh", "inner")


def shifted(value, axis, steps):
    count = lax.axis_size(axis)
    leading, last = (max(0, -steps), min(count, count - steps))
    return lax.ppermute(value, axis, [(source, source + steps) for source in range(leading, last)])


def main_diagonal(matrix):
    positions = np.arange(matrix.shape[0])
    return matrix[positions, positions]


def build_tables():
    line_stiff = np.array(
        [
            [1.0, -1.0, 0.0, 0.0],
            [-1.0, 2.0, -1.0, 0.0],
            [0.0, -1.0, 2.0, -1.0],
            [0.0, 0.0, -1.0, 1.0],
        ]
    )
    identity = np.eye(4)
    stiffness = (
        np.kron(np.kron(line_stiff, identity), identity)
        + np.kron(np.kron(identity, line_stiff), identity)
        + np.kron(np.kron(identity, identity), line_stiff)
    )
    ramp_basis = np.array([[1.0, 0.0], [2.0 / 3.0, 1.0 / 3.0], [1.0 / 3.0, 2.0 / 3.0], [0.0, 1.0]])
    prolong = np.kron(np.kron(ramp_basis, ramp_basis), ramp_basis)
    coarse_stiff = prolong.T @ stiffness @ prolong
    small_mass = ramp_basis.T @ ramp_basis
    face_mass = np.kron(small_mass, small_mass)
    return (stiffness, prolong, coarse_stiff, face_mass)


def face_slices(points):
    grid_ids = np.arange(points**3).reshape(points, points, points)
    last_index = points - 1
    return [
        grid_ids[0],
        grid_ids[last_index],
        grid_ids[:, 0],
        grid_ids[:, last_index],
        grid_ids[:, :, 0],
        grid_ids[:, :, last_index],
    ]


def lifting(points, face_mat):
    node_total = points**3
    per_face = points * points
    slices = face_slices(points)
    result = np.zeros((node_total, 6 * per_face))
    for face in range(6):
        select = np.zeros((node_total, per_face))
        select[slices[face].ravel(), np.arange(per_face)] = 1.0
        result[:, face * per_face : (face + 1) * per_face] = PENALTY * (select @ face_mat)
    return result


def face_diagonal(points, face_mat):
    result = np.zeros(points**3)
    for face_ids in face_slices(points):
        result[face_ids.ravel()] += PENALTY * main_diagonal(face_mat)
    return result


def stiff_and_traces(stiff, points):
    node_total = points**3
    per_face = points * points
    select = np.zeros((6 * per_face, node_total))
    for face, ids in enumerate(face_slices(points)):
        select[face * per_face + np.arange(per_face), ids.ravel()] = 1.0
    return np.concatenate([stiff, select], axis=0)


def shift_columns(values, offset):
    rows, width = values.shape
    pad = jnp.zeros((rows, abs(offset)), values.dtype)
    if offset > 0:
        return jnp.concatenate([values[:, offset:], pad], axis=1)
    return jnp.concatenate([pad, values[:, : width + offset]], axis=1)


def snake_places(mesh_size, inner_size, y_size=4, cores=2):
    places = np.zeros(mesh_size * inner_size, np.int64)
    for slab in range(mesh_size * inner_size):
        row, inner = divmod(slab, inner_size)
        z, rest = divmod(row, y_size * cores)
        y, core = divmod(rest, cores)
        x_place = inner if core % 2 == 0 else inner_size - 1 - inner
        y_place = y if z % 2 == 0 else y_size - 1 - y
        places[slab] = ((z * y_size + y_place) * cores + core) * inner_size + x_place
    return places


def scale_of(level):
    return 96.0 * PENALTY * (8.0 * 2.0**level) ** (2.0 / 3.0)


def local(source, density, neighbours, halo_sends, aggregate, partner_map):
    stiffness, prolong, coarse_stiff, face_mass = build_tables()
    big_fine = jnp.asarray(stiff_and_traces(stiffness, 4), jnp.float32)
    big_lin = jnp.asarray(stiff_and_traces(coarse_stiff, 2), jnp.float32)
    prolong_mat = jnp.asarray(prolong, jnp.float32)
    lift_fine = jnp.asarray(lifting(4, np.eye(16)), jnp.float32)
    lift_lin = jnp.asarray(lifting(2, face_mass), jnp.float32)
    diag_fine_k = jnp.asarray(main_diagonal(stiffness), jnp.float32)
    diag_fine_f = jnp.asarray(face_diagonal(4, np.eye(16)), jnp.float32)
    diag_lin_k = jnp.asarray(main_diagonal(coarse_stiff), jnp.float32)
    diag_lin_f = jnp.asarray(face_diagonal(2, face_mass), jnp.float32)
    elements = source.shape[1]
    layer = halo_sends.shape[1]
    groups_width = elements // 8

    ordering = jnp.concatenate([halo_sends[0], halo_sends[1]])
    to_brick = (
        jnp.arange(elements, dtype=jnp.int32)[:, None] == ordering[None, :]
    ).astype(jnp.float32)
    stacked_inputs = jnp.concatenate(
        [source, density[None, :], aggregate.astype(jnp.float32)[None, :]], axis=0
    )
    bundle = jnp.dot(stacked_inputs, to_brick, precision=PRECISE)

    devices = lax.axis_size("mesh") * lax.axis_size("inner")
    places = snake_places(lax.axis_size("mesh"), lax.axis_size("inner"))
    slab_of = np.argsort(places)
    here = lax.axis_index("mesh") * lax.axis_size("inner") + lax.axis_index("inner")
    flat_index = jnp.asarray(slab_of, jnp.int32)[here]
    bundle = lax.ppermute(bundle, AXES, [(q, int(places[q])) for q in range(devices)])
    rhs = bundle[:-2]
    dens = bundle[-2]
    agg = jnp.round(bundle[-1]).astype(jnp.int32)
    up_pairs = [(int(places[d]), int(places[d + 1])) for d in range(devices - 1)]
    down_pairs = [(b, a) for a, b in up_pairs]

    last_x = layer // BRICK_Y - 1
    runtime_zero = lax.optimization_barrier(jnp.zeros((), jnp.int32))

    def wall_masks(width):
        column = lax.broadcasted_iota(jnp.int32, (1, width), 1) + runtime_zero
        pos_x = column % layer // BRICK_Y
        pos_y = column % BRICK_Y
        return [pos_x > 0, pos_x < last_x, pos_y > 0, pos_y < BRICK_Y - 1]

    masks = wall_masks(elements)
    offsets = [-BRICK_Y, BRICK_Y, -1, 1]

    diag_fine = dens[None, :] * diag_fine_k[:, None] + diag_fine_f[:, None]
    diag_lin = dens[None, :] * diag_lin_k[:, None] + diag_lin_f[:, None]

    def apply(nodal_field, big, lift, node_total, per_face):
        stacked = jnp.dot(big, nodal_field, precision=PRECISE)
        stiff_part = stacked[:node_total]
        traces = [
            stacked[node_total + f * per_face : node_total + (f + 1) * per_face] for f in range(6)
        ]
        rim_low = lax.ppermute(traces[5][:, layer:], AXES, up_pairs)
        rim_high = lax.ppermute(traces[4][:, :layer], AXES, down_pairs)
        jumps = []
        for face in range(4):
            other = shift_columns(traces[face ^ 1], offsets[face])
            jumps.append(traces[face] - jnp.where(masks[face], other, 0.0))
        jumps.append(traces[4] - jnp.concatenate([rim_low, traces[5][:, :layer]], axis=1))
        jumps.append(traces[5] - jnp.concatenate([traces[4][:, layer:], rim_high], axis=1))
        jumps = jnp.concatenate(jumps, axis=0)
        return dens[None, :] * stiff_part + jnp.dot(lift, jumps, precision=PRECISE)

    wide_masks = wall_masks(3 * elements)

    def apply_wide(nodal_field, wide_dens):
        stacked = jnp.dot(big_lin, nodal_field, precision=PRECISE)
        stiff_part = stacked[:8]
        traces = [stacked[8 + f * 4 : 8 + (f + 1) * 4] for f in range(6)]
        jumps = []
        for face in range(4):
            other = shift_columns(traces[face ^ 1], offsets[face])
            jumps.append(traces[face] - jnp.where(wide_masks[face], other, 0.0))
        jumps.append(traces[4] - shift_columns(traces[5], -layer))
        jumps.append(traces[5] - shift_columns(traces[4], layer))
        jumps = jnp.concatenate(jumps, axis=0)
        return wide_dens[None, :] * stiff_part + jnp.dot(lift_lin, jumps, precision=PRECISE)

    def apply_fine(nodal_field):
        return apply(nodal_field, big_fine, lift_fine, 64, 16)

    def apply_lin(nodal_field):
        return apply(nodal_field, big_lin, lift_lin, 8, 4)

    solution = FINE_WEIGHT * rhs / diag_fine
    for sweep in range(SMOOTH_FINE - 1):
        solution = solution + FINE_WEIGHT * (rhs - apply_fine(solution)) / diag_fine
    resid_fine = rhs - apply_fine(solution)
    resid_lin = jnp.dot(prolong_mat.T, resid_fine, precision=PRECISE)
    assert SMOOTH_LIN <= 2
    own = slice(elements, 2 * elements)
    slab = jnp.concatenate([resid_lin, dens[None, :]], axis=0)
    below = lax.ppermute(slab, AXES, up_pairs)
    above = lax.ppermute(slab, AXES, down_pairs)
    wide_resid = jnp.concatenate([below[:-1], resid_lin, above[:-1]], axis=1)
    wide_dens = jnp.concatenate([below[-1], dens, above[-1]])
    wide_diag = wide_dens[None, :] * diag_lin_k[:, None] + diag_lin_f[:, None]
    keep = jnp.concatenate(
        [
            jnp.full((elements,), flat_index > 0),
            jnp.ones((elements,), bool),
            jnp.full((elements,), flat_index < devices - 1),
        ]
    )[None, :]
    wide = LINEAR_WEIGHT * wide_resid / wide_diag
    for sweep in range(SMOOTH_LIN - 1):
        wide = wide + LINEAR_WEIGHT * (wide_resid - apply_wide(wide, wide_dens)) / wide_diag
        wide = jnp.where(keep, wide, 0.0)
    left_lin = resid_lin - apply_wide(wide, wide_dens)[:, own]
    linear = wide[:, own]
    resid_elem = jnp.sum(left_lin, axis=0)

    group_ids = jnp.arange(groups_width, dtype=jnp.int32)
    agg_hot = agg[:, None] == group_ids[None, :]
    own_sums = jnp.sum(jnp.where(agg_hot, resid_elem[:, None], 0.0), axis=0)

    current = own_sums
    descent = []
    level = 0
    while 2**level < devices:
        pairs = [(int(places[d]), int(places[d ^ (1 << level)])) for d in range(devices)]
        partner = lax.ppermute(current, AXES, pairs)
        below_term = current / scale_of(level)
        is_lower = (flat_index >> level) % 2 == 0
        paired = jnp.where(
            is_lower, jnp.concatenate([current, partner]), jnp.concatenate([partner, current])
        )
        level += 1
        row_index = flat_index // 2**level * 2**level + (2 ** (level - 1) - 1)
        parents = lax.dynamic_index_in_dim(partner_map, row_index, 0, keepdims=False)
        hot = parents[:, None] == group_ids[None, :]
        current = jnp.sum(jnp.where(hot, paired[:, None], 0.0), axis=0)
        descent.append((hot, is_lower, below_term))
    total = current / scale_of(level)
    for hot, is_lower, below_term in reversed(descent):
        children = jnp.sum(jnp.where(hot, total[None, :], 0.0), axis=1)
        total = (
            jnp.where(is_lower, children[:groups_width], children[groups_width:]) + below_term
        )
    own_total = total
    coarse = resid_elem / (96.0 * PENALTY) + jnp.sum(
        jnp.where(agg_hot, own_total[None, :], 0.0), axis=1
    )

    linear = linear + coarse[None, :]
    wide = jnp.concatenate(
        [
            lax.ppermute(linear, AXES, up_pairs),
            linear,
            lax.ppermute(linear, AXES, down_pairs),
        ],
        axis=1,
    )
    for sweep in range(SMOOTH_LIN):
        wide = wide + LINEAR_WEIGHT * (wide_resid - apply_wide(wide, wide_dens)) / wide_diag
        wide = jnp.where(keep, wide, 0.0)
    linear = wide[:, own]
    solution = solution + jnp.dot(prolong_mat, linear, precision=PRECISE)
    for sweep in range(SMOOTH_FINE):
        solution = solution + FINE_WEIGHT * (rhs - apply_fine(solution)) / diag_fine
    result = jnp.concatenate([solution, coarse[None, :]], axis=0)
    result = lax.ppermute(result, AXES, [(int(places[d]), d) for d in range(devices)])
    result = lax.dot_general(
        result, to_brick, (((1,), (1,)), ((), ())), precision=PRECISE
    )
    return (result[:-1], result[-1])


def solution(mesh):
    return jax.shard_map(
        local,
        mesh=mesh,
        in_specs=(
            P(None, ("mesh", "inner")),
            P(("mesh", "inner")),
            P(None, ("mesh", "inner")),
            P(None, ("mesh", "inner")),
            P(("mesh", "inner")),
            P(),
        ),
        out_specs=(P(None, ("mesh", "inner")), P(("mesh", "inner"))),
        check_vma=False,
    )
```

```python
import jax
import jax.numpy as jnp
import numpy as np
from jax import lax
from jax.sharding import PartitionSpec as P

SMOOTH_FINE = 3
SMOOTH_LIN = 2
BRICK_Y = 8

PENALTY = 2.0
FINE_WEIGHT = 0.6
LINEAR_WEIGHT = 0.5
PRECISE = lax.Precision.HIGHEST
AXES = ("mesh", "inner")


def shifted(value, axis, steps):
    count = lax.axis_size(axis)
    leading, last = (max(0, -steps), min(count, count - steps))
    return lax.ppermute(value, axis, [(source, source + steps) for source in range(leading, last)])


def main_diagonal(matrix):
    positions = np.arange(matrix.shape[0])
    return matrix[positions, positions]


def build_tables():
    line_stiff = np.array(
        [
            [1.0, -1.0, 0.0, 0.0],
            [-1.0, 2.0, -1.0, 0.0],
            [0.0, -1.0, 2.0, -1.0],
            [0.0, 0.0, -1.0, 1.0],
        ]
    )
    identity = np.eye(4)
    stiffness = (
        np.kron(np.kron(line_stiff, identity), identity)
        + np.kron(np.kron(identity, line_stiff), identity)
        + np.kron(np.kron(identity, identity), line_stiff)
    )
    ramp_basis = np.array([[1.0, 0.0], [2.0 / 3.0, 1.0 / 3.0], [1.0 / 3.0, 2.0 / 3.0], [0.0, 1.0]])
    prolong = np.kron(np.kron(ramp_basis, ramp_basis), ramp_basis)
    coarse_stiff = prolong.T @ stiffness @ prolong
    small_mass = ramp_basis.T @ ramp_basis
    face_mass = np.kron(small_mass, small_mass)
    return (stiffness, prolong, coarse_stiff, face_mass)


def face_slices(points):
    grid_ids = np.arange(points**3).reshape(points, points, points)
    last_index = points - 1
    return [
        grid_ids[0],
        grid_ids[last_index],
        grid_ids[:, 0],
        grid_ids[:, last_index],
        grid_ids[:, :, 0],
        grid_ids[:, :, last_index],
    ]


def lifting(points, face_mat):
    node_total = points**3
    per_face = points * points
    slices = face_slices(points)
    result = np.zeros((node_total, 6 * per_face))
    for face in range(6):
        select = np.zeros((node_total, per_face))
        select[slices[face].ravel(), np.arange(per_face)] = 1.0
        result[:, face * per_face : (face + 1) * per_face] = PENALTY * (select @ face_mat)
    return result


def face_diagonal(points, face_mat):
    result = np.zeros(points**3)
    for face_ids in face_slices(points):
        result[face_ids.ravel()] += PENALTY * main_diagonal(face_mat)
    return result


def stiff_and_traces(stiff, points):
    node_total = points**3
    per_face = points * points
    select = np.zeros((6 * per_face, node_total))
    for face, ids in enumerate(face_slices(points)):
        select[face * per_face + np.arange(per_face), ids.ravel()] = 1.0
    return np.concatenate([stiff, select], axis=0)


def shift_columns(values, offset):
    rows, width = values.shape
    pad = jnp.zeros((rows, abs(offset)), values.dtype)
    if offset > 0:
        return jnp.concatenate([values[:, offset:], pad], axis=1)
    return jnp.concatenate([pad, values[:, : width + offset]], axis=1)


def snake_places(mesh_size, inner_size, y_size=4, cores=2):
    places = np.zeros(mesh_size * inner_size, np.int64)
    for slab in range(mesh_size * inner_size):
        row, inner = divmod(slab, inner_size)
        z, rest = divmod(row, y_size * cores)
        y, core = divmod(rest, cores)
        x_place = inner if core % 2 == 0 else inner_size - 1 - inner
        y_place = y if z % 2 == 0 else y_size - 1 - y
        places[slab] = ((z * y_size + y_place) * cores + core) * inner_size + x_place
    return places


def scale_of(level):
    return 96.0 * PENALTY * (8.0 * 2.0**level) ** (2.0 / 3.0)


def local(source, density, neighbours, halo_sends, aggregate, partner_map):
    stiffness, prolong, coarse_stiff, face_mass = build_tables()
    big_fine = jnp.asarray(stiff_and_traces(stiffness, 4), jnp.float32)
    big_lin = jnp.asarray(stiff_and_traces(coarse_stiff, 2), jnp.float32)
    prolong_mat = jnp.asarray(prolong, jnp.float32)
    lift_fine = jnp.asarray(lifting(4, np.eye(16)), jnp.float32)
    lift_lin = jnp.asarray(lifting(2, face_mass), jnp.float32)
    diag_fine_k = jnp.asarray(main_diagonal(stiffness), jnp.float32)
    diag_fine_f = jnp.asarray(face_diagonal(4, np.eye(16)), jnp.float32)
    diag_lin_k = jnp.asarray(main_diagonal(coarse_stiff), jnp.float32)
    diag_lin_f = jnp.asarray(face_diagonal(2, face_mass), jnp.float32)
    elements = source.shape[1]
    layer = halo_sends.shape[1]
    groups_width = elements // 8

    ordering = jnp.concatenate([halo_sends[0], halo_sends[1]])
    to_brick = (
        jnp.arange(elements, dtype=jnp.int32)[:, None] == ordering[None, :]
    ).astype(jnp.float32)
    stacked_inputs = jnp.concatenate(
        [source, density[None, :], aggregate.astype(jnp.float32)[None, :]], axis=0
    )
    bundle = jnp.dot(stacked_inputs, to_brick, precision=PRECISE)

    devices = lax.axis_size("mesh") * lax.axis_size("inner")
    places = snake_places(lax.axis_size("mesh"), lax.axis_size("inner"))
    slab_of = np.argsort(places)
    here = lax.axis_index("mesh") * lax.axis_size("inner") + lax.axis_index("inner")
    flat_index = jnp.asarray(slab_of, jnp.int32)[here]
    bundle = lax.ppermute(bundle, AXES, [(q, int(places[q])) for q in range(devices)])
    (
        big_fine, big_lin, prolong_mat, lift_fine, lift_lin,
        diag_fine_k, diag_fine_f, diag_lin_k, diag_lin_f, partner_map,
    ) = lax.optimization_barrier((
        big_fine, big_lin, prolong_mat, lift_fine, lift_lin,
        diag_fine_k, diag_fine_f, diag_lin_k, diag_lin_f, partner_map,
    ))
    rhs = bundle[:-2]
    dens = bundle[-2]
    agg = jnp.round(bundle[-1]).astype(jnp.int32)
    up_pairs = [(int(places[d]), int(places[d + 1])) for d in range(devices - 1)]
    down_pairs = [(b, a) for a, b in up_pairs]

    last_x = layer // BRICK_Y - 1
    runtime_zero = lax.optimization_barrier(jnp.zeros((), jnp.int32))

    def wall_masks(width):
        column = lax.broadcasted_iota(jnp.int32, (1, width), 1) + runtime_zero
        pos_x = column % layer // BRICK_Y
        pos_y = column % BRICK_Y
        return [pos_x > 0, pos_x < last_x, pos_y > 0, pos_y < BRICK_Y - 1]

    masks = wall_masks(elements)
    offsets = [-BRICK_Y, BRICK_Y, -1, 1]

    diag_fine = dens[None, :] * diag_fine_k[:, None] + diag_fine_f[:, None]
    diag_lin = dens[None, :] * diag_lin_k[:, None] + diag_lin_f[:, None]

    def apply(nodal_field, big, lift, node_total, per_face):
        stacked = jnp.dot(big, nodal_field, precision=PRECISE)
        stiff_part = stacked[:node_total]
        traces = [
            stacked[node_total + f * per_face : node_total + (f + 1) * per_face] for f in range(6)
        ]
        rim_low = lax.ppermute(traces[5][:, layer:], AXES, up_pairs)
        rim_high = lax.ppermute(traces[4][:, :layer], AXES, down_pairs)
        jumps = []
        for face in range(4):
            other = shift_columns(traces[face ^ 1], offsets[face])
            jumps.append(traces[face] - jnp.where(masks[face], other, 0.0))
        jumps.append(traces[4] - jnp.concatenate([rim_low, traces[5][:, :layer]], axis=1))
        jumps.append(traces[5] - jnp.concatenate([traces[4][:, layer:], rim_high], axis=1))
        jumps = jnp.concatenate(jumps, axis=0)
        return dens[None, :] * stiff_part + jnp.dot(lift, jumps, precision=PRECISE)

    wide_masks = wall_masks(3 * elements)

    def apply_wide(nodal_field, wide_dens):
        stacked = jnp.dot(big_lin, nodal_field, precision=PRECISE)
        stiff_part = stacked[:8]
        traces = [stacked[8 + f * 4 : 8 + (f + 1) * 4] for f in range(6)]
        jumps = []
        for face in range(4):
            other = shift_columns(traces[face ^ 1], offsets[face])
            jumps.append(traces[face] - jnp.where(wide_masks[face], other, 0.0))
        jumps.append(traces[4] - shift_columns(traces[5], -layer))
        jumps.append(traces[5] - shift_columns(traces[4], layer))
        jumps = jnp.concatenate(jumps, axis=0)
        return wide_dens[None, :] * stiff_part + jnp.dot(lift_lin, jumps, precision=PRECISE)

    def apply_fine(nodal_field):
        return apply(nodal_field, big_fine, lift_fine, 64, 16)

    def apply_lin(nodal_field):
        return apply(nodal_field, big_lin, lift_lin, 8, 4)

    solution = FINE_WEIGHT * rhs / diag_fine
    for sweep in range(SMOOTH_FINE - 1):
        solution = solution + FINE_WEIGHT * (rhs - apply_fine(solution)) / diag_fine
    resid_fine = rhs - apply_fine(solution)
    resid_lin = jnp.dot(prolong_mat.T, resid_fine, precision=PRECISE)
    assert SMOOTH_LIN <= 2
    own = slice(elements, 2 * elements)
    slab = jnp.concatenate([resid_lin, dens[None, :]], axis=0)
    below = lax.ppermute(slab, AXES, up_pairs)
    above = lax.ppermute(slab, AXES, down_pairs)
    wide_resid = jnp.concatenate([below[:-1], resid_lin, above[:-1]], axis=1)
    wide_dens = jnp.concatenate([below[-1], dens, above[-1]])
    wide_diag = wide_dens[None, :] * diag_lin_k[:, None] + diag_lin_f[:, None]
    keep = jnp.concatenate(
        [
            jnp.full((elements,), flat_index > 0),
            jnp.ones((elements,), bool),
            jnp.full((elements,), flat_index < devices - 1),
        ]
    )[None, :]
    wide = LINEAR_WEIGHT * wide_resid / wide_diag
    for sweep in range(SMOOTH_LIN - 1):
        wide = wide + LINEAR_WEIGHT * (wide_resid - apply_wide(wide, wide_dens)) / wide_diag
        wide = jnp.where(keep, wide, 0.0)
    left_lin = resid_lin - apply_wide(wide, wide_dens)[:, own]
    linear = wide[:, own]
    resid_elem = jnp.sum(left_lin, axis=0)

    group_ids = jnp.arange(groups_width, dtype=jnp.int32)
    agg_hot = agg[:, None] == group_ids[None, :]
    own_sums = jnp.sum(jnp.where(agg_hot, resid_elem[:, None], 0.0), axis=0)

    current = own_sums
    descent = []
    level = 0
    while 2**level < devices:
        pairs = [(int(places[d]), int(places[d ^ (1 << level)])) for d in range(devices)]
        partner = lax.ppermute(current, AXES, pairs)
        below_term = current / scale_of(level)
        is_lower = (flat_index >> level) % 2 == 0
        paired = jnp.where(
            is_lower, jnp.concatenate([current, partner]), jnp.concatenate([partner, current])
        )
        level += 1
        row_index = flat_index // 2**level * 2**level + (2 ** (level - 1) - 1)
        parents = lax.dynamic_index_in_dim(partner_map, row_index, 0, keepdims=False)
        hot = parents[:, None] == group_ids[None, :]
        current = jnp.sum(jnp.where(hot, paired[:, None], 0.0), axis=0)
        descent.append((hot, is_lower, below_term))
    total = current / scale_of(level)
    for hot, is_lower, below_term in reversed(descent):
        children = jnp.sum(jnp.where(hot, total[None, :], 0.0), axis=1)
        total = (
            jnp.where(is_lower, children[:groups_width], children[groups_width:]) + below_term
        )
    own_total = total
    coarse = resid_elem / (96.0 * PENALTY) + jnp.sum(
        jnp.where(agg_hot, own_total[None, :], 0.0), axis=1
    )

    linear = linear + coarse[None, :]
    wide = jnp.concatenate(
        [
            lax.ppermute(linear, AXES, up_pairs),
            linear,
            lax.ppermute(linear, AXES, down_pairs),
        ],
        axis=1,
    )
    for sweep in range(SMOOTH_LIN):
        wide = wide + LINEAR_WEIGHT * (wide_resid - apply_wide(wide, wide_dens)) / wide_diag
        wide = jnp.where(keep, wide, 0.0)
    linear = wide[:, own]
    solution = solution + jnp.dot(prolong_mat, linear, precision=PRECISE)
    for sweep in range(SMOOTH_FINE):
        solution = solution + FINE_WEIGHT * (rhs - apply_fine(solution)) / diag_fine
    result = jnp.concatenate([solution, coarse[None, :]], axis=0)
    result = lax.ppermute(result, AXES, [(int(places[d]), d) for d in range(devices)])
    result = lax.dot_general(
        result, to_brick, (((1,), (1,)), ((), ())), precision=PRECISE
    )
    return (result[:-1], result[-1])


def solution(mesh):
    return jax.shard_map(
        local,
        mesh=mesh,
        in_specs=(
            P(None, ("mesh", "inner")),
            P(("mesh", "inner")),
            P(None, ("mesh", "inner")),
            P(None, ("mesh", "inner")),
            P(("mesh", "inner")),
            P(),
        ),
        out_specs=(P(None, ("mesh", "inner")), P(("mesh", "inner"))),
        check_vma=False,
    )
```

```python
import jax
import jax.numpy as jnp
import numpy as np
from jax import lax
from jax.sharding import PartitionSpec as P

SMOOTH_FINE = 3
SMOOTH_LIN = 2
BRICK_Y = 8

PENALTY = 2.0
FINE_WEIGHT = 0.6
LINEAR_WEIGHT = 0.5
PRECISE = lax.Precision.HIGHEST
AXES = ("mesh", "inner")


def shifted(value, axis, steps):
    count = lax.axis_size(axis)
    leading, last = (max(0, -steps), min(count, count - steps))
    return lax.ppermute(value, axis, [(source, source + steps) for source in range(leading, last)])


def main_diagonal(matrix):
    positions = np.arange(matrix.shape[0])
    return matrix[positions, positions]


def build_tables():
    line_stiff = np.array(
        [
            [1.0, -1.0, 0.0, 0.0],
            [-1.0, 2.0, -1.0, 0.0],
            [0.0, -1.0, 2.0, -1.0],
            [0.0, 0.0, -1.0, 1.0],
        ]
    )
    identity = np.eye(4)
    stiffness = (
        np.kron(np.kron(line_stiff, identity), identity)
        + np.kron(np.kron(identity, line_stiff), identity)
        + np.kron(np.kron(identity, identity), line_stiff)
    )
    ramp_basis = np.array([[1.0, 0.0], [2.0 / 3.0, 1.0 / 3.0], [1.0 / 3.0, 2.0 / 3.0], [0.0, 1.0]])
    prolong = np.kron(np.kron(ramp_basis, ramp_basis), ramp_basis)
    coarse_stiff = prolong.T @ stiffness @ prolong
    small_mass = ramp_basis.T @ ramp_basis
    face_mass = np.kron(small_mass, small_mass)
    return (stiffness, prolong, coarse_stiff, face_mass)


def face_slices(points):
    grid_ids = np.arange(points**3).reshape(points, points, points)
    last_index = points - 1
    return [
        grid_ids[0],
        grid_ids[last_index],
        grid_ids[:, 0],
        grid_ids[:, last_index],
        grid_ids[:, :, 0],
        grid_ids[:, :, last_index],
    ]


def lifting(points, face_mat):
    node_total = points**3
    per_face = points * points
    slices = face_slices(points)
    result = np.zeros((node_total, 6 * per_face))
    for face in range(6):
        select = np.zeros((node_total, per_face))
        select[slices[face].ravel(), np.arange(per_face)] = 1.0
        result[:, face * per_face : (face + 1) * per_face] = PENALTY * (select @ face_mat)
    return result


def face_diagonal(points, face_mat):
    result = np.zeros(points**3)
    for face_ids in face_slices(points):
        result[face_ids.ravel()] += PENALTY * main_diagonal(face_mat)
    return result


def stiff_and_traces(stiff, points):
    node_total = points**3
    per_face = points * points
    select = np.zeros((6 * per_face, node_total))
    for face, ids in enumerate(face_slices(points)):
        select[face * per_face + np.arange(per_face), ids.ravel()] = 1.0
    return np.concatenate([stiff, select], axis=0)


def shift_columns(values, offset):
    rows, width = values.shape
    pad = jnp.zeros((rows, abs(offset)), values.dtype)
    if offset > 0:
        return jnp.concatenate([values[:, offset:], pad], axis=1)
    return jnp.concatenate([pad, values[:, : width + offset]], axis=1)


def snake_places(mesh_size, inner_size, y_size=4, cores=2):
    places = np.zeros(mesh_size * inner_size, np.int64)
    for slab in range(mesh_size * inner_size):
        row, inner = divmod(slab, inner_size)
        z, rest = divmod(row, y_size * cores)
        y, core = divmod(rest, cores)
        x_place = inner if core % 2 == 0 else inner_size - 1 - inner
        y_place = y if z % 2 == 0 else y_size - 1 - y
        places[slab] = ((z * y_size + y_place) * cores + core) * inner_size + x_place
    return places


def scale_of(level):
    return 96.0 * PENALTY * (8.0 * 2.0**level) ** (2.0 / 3.0)


def local(source, density, neighbours, halo_sends, aggregate, partner_map):
    stiffness, prolong, coarse_stiff, face_mass = build_tables()
    big_fine = jnp.asarray(stiff_and_traces(stiffness, 4), jnp.float32)
    big_lin = jnp.asarray(stiff_and_traces(coarse_stiff, 2), jnp.float32)
    prolong_mat = jnp.asarray(prolong, jnp.float32)
    lift_fine = jnp.asarray(lifting(4, np.eye(16)), jnp.float32)
    lift_lin = jnp.asarray(lifting(2, face_mass), jnp.float32)
    diag_fine_k = jnp.asarray(main_diagonal(stiffness), jnp.float32)
    diag_fine_f = jnp.asarray(face_diagonal(4, np.eye(16)), jnp.float32)
    diag_lin_k = jnp.asarray(main_diagonal(coarse_stiff), jnp.float32)
    diag_lin_f = jnp.asarray(face_diagonal(2, face_mass), jnp.float32)
    elements = source.shape[1]
    layer = halo_sends.shape[1]
    groups_width = elements // 8

    ordering = jnp.concatenate([halo_sends[0], halo_sends[1]])
    bundle = jnp.concatenate(
        [
            source,
            density[None, :],
            aggregate.astype(jnp.float32)[None, :],
            ordering.astype(jnp.float32)[None, :],
        ],
        axis=0,
    )

    devices = lax.axis_size("mesh") * lax.axis_size("inner")
    places = snake_places(lax.axis_size("mesh"), lax.axis_size("inner"))
    slab_of = np.argsort(places)
    here = lax.axis_index("mesh") * lax.axis_size("inner") + lax.axis_index("inner")
    flat_index = jnp.asarray(slab_of, jnp.int32)[here]
    bundle = lax.ppermute(bundle, AXES, [(q, int(places[q])) for q in range(devices)])
    (
        big_fine, big_lin, prolong_mat, lift_fine, lift_lin,
        diag_fine_k, diag_fine_f, diag_lin_k, diag_lin_f, partner_map,
    ) = lax.optimization_barrier((
        big_fine, big_lin, prolong_mat, lift_fine, lift_lin,
        diag_fine_k, diag_fine_f, diag_lin_k, diag_lin_f, partner_map,
    ))
    to_brick = (
        jnp.arange(elements, dtype=jnp.int32)[:, None]
        == jnp.round(bundle[-1]).astype(jnp.int32)[None, :]
    ).astype(jnp.float32)
    bundle = jnp.dot(bundle[:-1], to_brick, precision=PRECISE)
    rhs = bundle[:-2]
    dens = bundle[-2]
    agg = jnp.round(bundle[-1]).astype(jnp.int32)
    up_pairs = [(int(places[d]), int(places[d + 1])) for d in range(devices - 1)]
    down_pairs = [(b, a) for a, b in up_pairs]

    last_x = layer // BRICK_Y - 1
    runtime_zero = lax.optimization_barrier(jnp.zeros((), jnp.int32))

    def wall_masks(width):
        column = lax.broadcasted_iota(jnp.int32, (1, width), 1) + runtime_zero
        pos_x = column % layer // BRICK_Y
        pos_y = column % BRICK_Y
        return [pos_x > 0, pos_x < last_x, pos_y > 0, pos_y < BRICK_Y - 1]

    masks = wall_masks(elements)
    offsets = [-BRICK_Y, BRICK_Y, -1, 1]

    diag_fine = dens[None, :] * diag_fine_k[:, None] + diag_fine_f[:, None]
    diag_lin = dens[None, :] * diag_lin_k[:, None] + diag_lin_f[:, None]

    def apply(nodal_field, big, lift, node_total, per_face):
        stacked = jnp.dot(big, nodal_field, precision=PRECISE)
        stiff_part = stacked[:node_total]
        traces = [
            stacked[node_total + f * per_face : node_total + (f + 1) * per_face] for f in range(6)
        ]
        rim_low = lax.ppermute(traces[5][:, layer:], AXES, up_pairs)
        rim_high = lax.ppermute(traces[4][:, :layer], AXES, down_pairs)
        jumps = []
        for face in range(4):
            other = shift_columns(traces[face ^ 1], offsets[face])
            jumps.append(traces[face] - jnp.where(masks[face], other, 0.0))
        jumps.append(traces[4] - jnp.concatenate([rim_low, traces[5][:, :layer]], axis=1))
        jumps.append(traces[5] - jnp.concatenate([traces[4][:, layer:], rim_high], axis=1))
        jumps = jnp.concatenate(jumps, axis=0)
        return dens[None, :] * stiff_part + jnp.dot(lift, jumps, precision=PRECISE)

    wide_masks = wall_masks(3 * elements)

    def apply_wide(nodal_field, wide_dens):
        stacked = jnp.dot(big_lin, nodal_field, precision=PRECISE)
        stiff_part = stacked[:8]
        traces = [stacked[8 + f * 4 : 8 + (f + 1) * 4] for f in range(6)]
        jumps = []
        for face in range(4):
            other = shift_columns(traces[face ^ 1], offsets[face])
            jumps.append(traces[face] - jnp.where(wide_masks[face], other, 0.0))
        jumps.append(traces[4] - shift_columns(traces[5], -layer))
        jumps.append(traces[5] - shift_columns(traces[4], layer))
        jumps = jnp.concatenate(jumps, axis=0)
        return wide_dens[None, :] * stiff_part + jnp.dot(lift_lin, jumps, precision=PRECISE)

    def apply_fine(nodal_field):
        return apply(nodal_field, big_fine, lift_fine, 64, 16)

    def apply_lin(nodal_field):
        return apply(nodal_field, big_lin, lift_lin, 8, 4)

    solution = FINE_WEIGHT * rhs / diag_fine
    for sweep in range(SMOOTH_FINE - 1):
        solution = solution + FINE_WEIGHT * (rhs - apply_fine(solution)) / diag_fine
    resid_fine = rhs - apply_fine(solution)
    resid_lin = jnp.dot(prolong_mat.T, resid_fine, precision=PRECISE)
    assert SMOOTH_LIN <= 2
    own = slice(elements, 2 * elements)
    slab = jnp.concatenate([resid_lin, dens[None, :]], axis=0)
    below = lax.ppermute(slab, AXES, up_pairs)
    above = lax.ppermute(slab, AXES, down_pairs)
    wide_resid = jnp.concatenate([below[:-1], resid_lin, above[:-1]], axis=1)
    wide_dens = jnp.concatenate([below[-1], dens, above[-1]])
    wide_diag = wide_dens[None, :] * diag_lin_k[:, None] + diag_lin_f[:, None]
    keep = jnp.concatenate(
        [
            jnp.full((elements,), flat_index > 0),
            jnp.ones((elements,), bool),
            jnp.full((elements,), flat_index < devices - 1),
        ]
    )[None, :]
    wide = LINEAR_WEIGHT * wide_resid / wide_diag
    for sweep in range(SMOOTH_LIN - 1):
        wide = wide + LINEAR_WEIGHT * (wide_resid - apply_wide(wide, wide_dens)) / wide_diag
        wide = jnp.where(keep, wide, 0.0)
    left_lin = resid_lin - apply_wide(wide, wide_dens)[:, own]
    linear = wide[:, own]
    resid_elem = jnp.sum(left_lin, axis=0)

    group_ids = jnp.arange(groups_width, dtype=jnp.int32)
    agg_hot = agg[:, None] == group_ids[None, :]
    own_sums = jnp.sum(jnp.where(agg_hot, resid_elem[:, None], 0.0), axis=0)

    current = own_sums
    descent = []
    level = 0
    while 2**level < devices:
        pairs = [(int(places[d]), int(places[d ^ (1 << level)])) for d in range(devices)]
        partner = lax.ppermute(current, AXES, pairs)
        below_term = current / scale_of(level)
        is_lower = (flat_index >> level) % 2 == 0
        paired = jnp.where(
            is_lower, jnp.concatenate([current, partner]), jnp.concatenate([partner, current])
        )
        level += 1
        row_index = flat_index // 2**level * 2**level + (2 ** (level - 1) - 1)
        parents = lax.dynamic_index_in_dim(partner_map, row_index, 0, keepdims=False)
        hot = parents[:, None] == group_ids[None, :]
        current = jnp.sum(jnp.where(hot, paired[:, None], 0.0), axis=0)
        descent.append((hot, is_lower, below_term))
    total = current / scale_of(level)
    for hot, is_lower, below_term in reversed(descent):
        children = jnp.sum(jnp.where(hot, total[None, :], 0.0), axis=1)
        total = (
            jnp.where(is_lower, children[:groups_width], children[groups_width:]) + below_term
        )
    own_total = total
    coarse = resid_elem / (96.0 * PENALTY) + jnp.sum(
        jnp.where(agg_hot, own_total[None, :], 0.0), axis=1
    )

    linear = linear + coarse[None, :]
    wide = jnp.concatenate(
        [
            lax.ppermute(linear, AXES, up_pairs),
            linear,
            lax.ppermute(linear, AXES, down_pairs),
        ],
        axis=1,
    )
    for sweep in range(SMOOTH_LIN):
        wide = wide + LINEAR_WEIGHT * (wide_resid - apply_wide(wide, wide_dens)) / wide_diag
        wide = jnp.where(keep, wide, 0.0)
    linear = wide[:, own]
    solution = solution + jnp.dot(prolong_mat, linear, precision=PRECISE)
    for sweep in range(SMOOTH_FINE):
        solution = solution + FINE_WEIGHT * (rhs - apply_fine(solution)) / diag_fine
    result = jnp.concatenate([solution, coarse[None, :]], axis=0)
    result = lax.dot_general(
        result, to_brick, (((1,), (1,)), ((), ())), precision=PRECISE
    )
    result = lax.ppermute(result, AXES, [(int(places[d]), d) for d in range(devices)])
    return (result[:-1], result[-1])


def solution(mesh):
    return jax.shard_map(
        local,
        mesh=mesh,
        in_specs=(
            P(None, ("mesh", "inner")),
            P(("mesh", "inner")),
            P(None, ("mesh", "inner")),
            P(None, ("mesh", "inner")),
            P(("mesh", "inner")),
            P(),
        ),
        out_specs=(P(None, ("mesh", "inner")), P(("mesh", "inner"))),
        check_vma=False,
    )
```

```python
import jax
import jax.numpy as jnp
import numpy as np
from jax import lax
from jax.sharding import PartitionSpec as P

SMOOTH_FINE = 3
SMOOTH_LIN = 2
BRICK_Y = 8

PENALTY = 2.0
FINE_WEIGHT = 0.6
LINEAR_WEIGHT = 0.5
PRECISE = lax.Precision.HIGHEST
AXES = ("mesh", "inner")


def shifted(value, axis, steps):
    count = lax.axis_size(axis)
    leading, last = (max(0, -steps), min(count, count - steps))
    return lax.ppermute(value, axis, [(source, source + steps) for source in range(leading, last)])


def main_diagonal(matrix):
    positions = np.arange(matrix.shape[0])
    return matrix[positions, positions]


def build_tables():
    line_stiff = np.array(
        [
            [1.0, -1.0, 0.0, 0.0],
            [-1.0, 2.0, -1.0, 0.0],
            [0.0, -1.0, 2.0, -1.0],
            [0.0, 0.0, -1.0, 1.0],
        ]
    )
    identity = np.eye(4)
    stiffness = (
        np.kron(np.kron(line_stiff, identity), identity)
        + np.kron(np.kron(identity, line_stiff), identity)
        + np.kron(np.kron(identity, identity), line_stiff)
    )
    ramp_basis = np.array([[1.0, 0.0], [2.0 / 3.0, 1.0 / 3.0], [1.0 / 3.0, 2.0 / 3.0], [0.0, 1.0]])
    prolong = np.kron(np.kron(ramp_basis, ramp_basis), ramp_basis)
    coarse_stiff = prolong.T @ stiffness @ prolong
    small_mass = ramp_basis.T @ ramp_basis
    face_mass = np.kron(small_mass, small_mass)
    return (stiffness, prolong, coarse_stiff, face_mass)


def face_slices(points):
    grid_ids = np.arange(points**3).reshape(points, points, points)
    last_index = points - 1
    return [
        grid_ids[0],
        grid_ids[last_index],
        grid_ids[:, 0],
        grid_ids[:, last_index],
        grid_ids[:, :, 0],
        grid_ids[:, :, last_index],
    ]


def lifting(points, face_mat):
    node_total = points**3
    per_face = points * points
    slices = face_slices(points)
    result = np.zeros((node_total, 6 * per_face))
    for face in range(6):
        select = np.zeros((node_total, per_face))
        select[slices[face].ravel(), np.arange(per_face)] = 1.0
        result[:, face * per_face : (face + 1) * per_face] = PENALTY * (select @ face_mat)
    return result


def face_diagonal(points, face_mat):
    result = np.zeros(points**3)
    for face_ids in face_slices(points):
        result[face_ids.ravel()] += PENALTY * main_diagonal(face_mat)
    return result


def stiff_and_traces(stiff, points):
    node_total = points**3
    per_face = points * points
    select = np.zeros((6 * per_face, node_total))
    for face, ids in enumerate(face_slices(points)):
        select[face * per_face + np.arange(per_face), ids.ravel()] = 1.0
    return np.concatenate([stiff, select], axis=0)


def shift_columns(values, offset):
    rows, width = values.shape
    pad = jnp.zeros((rows, abs(offset)), values.dtype)
    if offset > 0:
        return jnp.concatenate([values[:, offset:], pad], axis=1)
    return jnp.concatenate([pad, values[:, : width + offset]], axis=1)


def snake_places(mesh_size, inner_size, y_size=4, cores=2):
    places = np.zeros(mesh_size * inner_size, np.int64)
    for slab in range(mesh_size * inner_size):
        row, inner = divmod(slab, inner_size)
        z, rest = divmod(row, y_size * cores)
        y, core = divmod(rest, cores)
        x_place = inner if core % 2 == 0 else inner_size - 1 - inner
        y_place = y if z % 2 == 0 else y_size - 1 - y
        places[slab] = ((z * y_size + y_place) * cores + core) * inner_size + x_place
    return places


def scale_of(level):
    return 96.0 * PENALTY * (8.0 * 2.0**level) ** (2.0 / 3.0)


def local(source, density, neighbours, halo_sends, aggregate, partner_map):
    stiffness, prolong, coarse_stiff, face_mass = build_tables()
    big_fine = jnp.asarray(stiff_and_traces(stiffness, 4), jnp.float32)
    big_lin = jnp.asarray(stiff_and_traces(coarse_stiff, 2), jnp.float32)
    prolong_mat = jnp.asarray(prolong, jnp.float32)
    lift_fine = jnp.asarray(lifting(4, np.eye(16)), jnp.float32)
    lift_lin = jnp.asarray(lifting(2, face_mass), jnp.float32)
    diag_fine_k = jnp.asarray(main_diagonal(stiffness), jnp.float32)
    diag_fine_f = jnp.asarray(face_diagonal(4, np.eye(16)), jnp.float32)
    diag_lin_k = jnp.asarray(main_diagonal(coarse_stiff), jnp.float32)
    diag_lin_f = jnp.asarray(face_diagonal(2, face_mass), jnp.float32)
    elements = source.shape[1]
    layer = halo_sends.shape[1]
    groups_width = elements // 8

    ordering = jnp.concatenate([halo_sends[0], halo_sends[1]])
    to_brick = (
        jnp.arange(elements, dtype=jnp.int32)[:, None] == ordering[None, :]
    ).astype(jnp.float32)
    stacked_inputs = jnp.concatenate(
        [source, density[None, :], aggregate.astype(jnp.float32)[None, :]], axis=0
    )
    bundle = jnp.dot(stacked_inputs, to_brick, precision=PRECISE)

    devices = lax.axis_size("mesh") * lax.axis_size("inner")
    places = snake_places(lax.axis_size("mesh"), lax.axis_size("inner"))
    slab_of = np.argsort(places)
    here = lax.axis_index("mesh") * lax.axis_size("inner") + lax.axis_index("inner")
    flat_index = jnp.asarray(slab_of, jnp.int32)[here]
    bundle = lax.ppermute(bundle, AXES, [(q, int(places[q])) for q in range(devices)])
    (
        big_fine, big_lin, prolong_mat, lift_fine, lift_lin,
        diag_fine_k, diag_fine_f, diag_lin_k, diag_lin_f, partner_map,
    ) = lax.optimization_barrier((
        big_fine, big_lin, prolong_mat, lift_fine, lift_lin,
        diag_fine_k, diag_fine_f, diag_lin_k, diag_lin_f, partner_map,
    ))
    rhs = bundle[:-2]
    dens = bundle[-2]
    agg = jnp.round(bundle[-1]).astype(jnp.int32)
    up_pairs = [(int(places[d]), int(places[d + 1])) for d in range(devices - 1)]
    down_pairs = [(b, a) for a, b in up_pairs]

    last_x = layer // BRICK_Y - 1
    runtime_zero = lax.optimization_barrier(jnp.zeros((), jnp.int32))

    def wall_masks(width):
        column = lax.broadcasted_iota(jnp.int32, (1, width), 1) + runtime_zero
        pos_x = column % layer // BRICK_Y
        pos_y = column % BRICK_Y
        return [pos_x > 0, pos_x < last_x, pos_y > 0, pos_y < BRICK_Y - 1]

    masks = wall_masks(elements)
    offsets = [-BRICK_Y, BRICK_Y, -1, 1]

    diag_fine = dens[None, :] * diag_fine_k[:, None] + diag_fine_f[:, None]
    diag_lin = dens[None, :] * diag_lin_k[:, None] + diag_lin_f[:, None]

    def apply(nodal_field, big, lift, node_total, per_face):
        stacked = jnp.dot(big, nodal_field, precision=PRECISE)
        stiff_part = stacked[:node_total]
        traces = [
            stacked[node_total + f * per_face : node_total + (f + 1) * per_face] for f in range(6)
        ]
        rim_low = lax.ppermute(traces[5][:, layer:], AXES, up_pairs)
        rim_high = lax.ppermute(traces[4][:, :layer], AXES, down_pairs)
        jumps = []
        for face in range(4):
            other = shift_columns(traces[face ^ 1], offsets[face])
            jumps.append(traces[face] - jnp.where(masks[face], other, 0.0))
        jumps.append(traces[4] - jnp.concatenate([rim_low, traces[5][:, :layer]], axis=1))
        jumps.append(traces[5] - jnp.concatenate([traces[4][:, layer:], rim_high], axis=1))
        jumps = jnp.concatenate(jumps, axis=0)
        return dens[None, :] * stiff_part + jnp.dot(lift, jumps, precision=PRECISE)

    wide_masks = wall_masks(3 * elements)

    def apply_wide(nodal_field, wide_dens, big=None, lift=None, node_total=8, per_face=4):
        big = big_lin if big is None else big
        lift = lift_lin if lift is None else lift
        stacked = jnp.dot(big, nodal_field, precision=PRECISE)
        stiff_part = stacked[:node_total]
        traces = [
            stacked[node_total + f * per_face : node_total + (f + 1) * per_face] for f in range(6)
        ]
        jumps = []
        for face in range(4):
            other = shift_columns(traces[face ^ 1], offsets[face])
            jumps.append(traces[face] - jnp.where(wide_masks[face], other, 0.0))
        jumps.append(traces[4] - shift_columns(traces[5], -layer))
        jumps.append(traces[5] - shift_columns(traces[4], layer))
        jumps = jnp.concatenate(jumps, axis=0)
        return wide_dens[None, :] * stiff_part + jnp.dot(lift, jumps, precision=PRECISE)

    def apply_fine(nodal_field):
        return apply(nodal_field, big_fine, lift_fine, 64, 16)

    def apply_lin(nodal_field):
        return apply(nodal_field, big_lin, lift_lin, 8, 4)

    assert SMOOTH_FINE - 1 <= 2
    own = slice(elements, 2 * elements)
    keep = jnp.concatenate(
        [
            jnp.full((elements,), flat_index > 0),
            jnp.ones((elements,), bool),
            jnp.full((elements,), flat_index < devices - 1),
        ]
    )[None, :]
    fine_slab = jnp.concatenate([rhs, dens[None, :]], axis=0)
    below_fine = lax.ppermute(fine_slab, AXES, up_pairs)
    above_fine = lax.ppermute(fine_slab, AXES, down_pairs)
    wide_rhs = jnp.concatenate([below_fine[:-1], rhs, above_fine[:-1]], axis=1)
    wide_dens_fine = jnp.concatenate([below_fine[-1], dens, above_fine[-1]])
    wide_diag_fine = wide_dens_fine[None, :] * diag_fine_k[:, None] + diag_fine_f[:, None]
    wide = jnp.where(keep, FINE_WEIGHT * wide_rhs / wide_diag_fine, 0.0)
    for sweep in range(SMOOTH_FINE - 1):
        wide_applied = apply_wide(wide, wide_dens_fine, big_fine, lift_fine, 64, 16)
        wide = wide + FINE_WEIGHT * (wide_rhs - wide_applied) / wide_diag_fine
        wide = jnp.where(keep, wide, 0.0)
    solution = wide[:, own]
    resid_fine = rhs - apply_fine(solution)
    resid_lin = jnp.dot(prolong_mat.T, resid_fine, precision=PRECISE)
    assert SMOOTH_LIN <= 2
    slab = jnp.concatenate([resid_lin, dens[None, :]], axis=0)
    below = lax.ppermute(slab, AXES, up_pairs)
    above = lax.ppermute(slab, AXES, down_pairs)
    wide_resid = jnp.concatenate([below[:-1], resid_lin, above[:-1]], axis=1)
    wide_dens = jnp.concatenate([below[-1], dens, above[-1]])
    wide_diag = wide_dens[None, :] * diag_lin_k[:, None] + diag_lin_f[:, None]
    wide = LINEAR_WEIGHT * wide_resid / wide_diag
    for sweep in range(SMOOTH_LIN - 1):
        wide = wide + LINEAR_WEIGHT * (wide_resid - apply_wide(wide, wide_dens)) / wide_diag
        wide = jnp.where(keep, wide, 0.0)
    left_lin = resid_lin - apply_wide(wide, wide_dens)[:, own]
    linear = wide[:, own]
    resid_elem = jnp.sum(left_lin, axis=0)

    group_ids = jnp.arange(groups_width, dtype=jnp.int32)
    agg_hot = agg[:, None] == group_ids[None, :]
    own_sums = jnp.sum(jnp.where(agg_hot, resid_elem[:, None], 0.0), axis=0)

    current = own_sums
    descent = []
    level = 0
    while 2**level < devices:
        pairs = [(int(places[d]), int(places[d ^ (1 << level)])) for d in range(devices)]
        partner = lax.ppermute(current, AXES, pairs)
        below_term = current / scale_of(level)
        is_lower = (flat_index >> level) % 2 == 0
        paired = jnp.where(
            is_lower, jnp.concatenate([current, partner]), jnp.concatenate([partner, current])
        )
        level += 1
        row_index = flat_index // 2**level * 2**level + (2 ** (level - 1) - 1)
        parents = lax.dynamic_index_in_dim(partner_map, row_index, 0, keepdims=False)
        hot = parents[:, None] == group_ids[None, :]
        current = jnp.sum(jnp.where(hot, paired[:, None], 0.0), axis=0)
        descent.append((hot, is_lower, below_term))
    total = current / scale_of(level)
    for hot, is_lower, below_term in reversed(descent):
        children = jnp.sum(jnp.where(hot, total[None, :], 0.0), axis=1)
        total = (
            jnp.where(is_lower, children[:groups_width], children[groups_width:]) + below_term
        )
    own_total = total
    coarse = resid_elem / (96.0 * PENALTY) + jnp.sum(
        jnp.where(agg_hot, own_total[None, :], 0.0), axis=1
    )

    linear = linear + coarse[None, :]
    wide = jnp.concatenate(
        [
            lax.ppermute(linear, AXES, up_pairs),
            linear,
            lax.ppermute(linear, AXES, down_pairs),
        ],
        axis=1,
    )
    for sweep in range(SMOOTH_LIN):
        wide = wide + LINEAR_WEIGHT * (wide_resid - apply_wide(wide, wide_dens)) / wide_diag
        wide = jnp.where(keep, wide, 0.0)
    linear = wide[:, own]
    solution = solution + jnp.dot(prolong_mat, linear, precision=PRECISE)
    for sweep in range(SMOOTH_FINE):
        solution = solution + FINE_WEIGHT * (rhs - apply_fine(solution)) / diag_fine
    result = jnp.concatenate([solution, coarse[None, :]], axis=0)
    result = lax.ppermute(result, AXES, [(int(places[d]), d) for d in range(devices)])
    result = lax.dot_general(
        result, to_brick, (((1,), (1,)), ((), ())), precision=PRECISE
    )
    return (result[:-1], result[-1])


def solution(mesh):
    return jax.shard_map(
        local,
        mesh=mesh,
        in_specs=(
            P(None, ("mesh", "inner")),
            P(("mesh", "inner")),
            P(None, ("mesh", "inner")),
            P(None, ("mesh", "inner")),
            P(("mesh", "inner")),
            P(),
        ),
        out_specs=(P(None, ("mesh", "inner")), P(("mesh", "inner"))),
        check_vma=False,
    )
```

```python
import jax
import jax.numpy as jnp
import numpy as np
from jax import lax
from jax.sharding import PartitionSpec as P

SMOOTH_FINE = 3
SMOOTH_LIN = 2
BRICK_Y = 8

PENALTY = 2.0
FINE_WEIGHT = 0.6
LINEAR_WEIGHT = 0.5
PRECISE = lax.Precision.HIGHEST
AXES = ("mesh", "inner")


def shifted(value, axis, steps):
    count = lax.axis_size(axis)
    leading, last = (max(0, -steps), min(count, count - steps))
    return lax.ppermute(value, axis, [(source, source + steps) for source in range(leading, last)])


def main_diagonal(matrix):
    positions = np.arange(matrix.shape[0])
    return matrix[positions, positions]


def build_tables():
    line_stiff = np.array(
        [
            [1.0, -1.0, 0.0, 0.0],
            [-1.0, 2.0, -1.0, 0.0],
            [0.0, -1.0, 2.0, -1.0],
            [0.0, 0.0, -1.0, 1.0],
        ]
    )
    identity = np.eye(4)
    stiffness = (
        np.kron(np.kron(line_stiff, identity), identity)
        + np.kron(np.kron(identity, line_stiff), identity)
        + np.kron(np.kron(identity, identity), line_stiff)
    )
    ramp_basis = np.array([[1.0, 0.0], [2.0 / 3.0, 1.0 / 3.0], [1.0 / 3.0, 2.0 / 3.0], [0.0, 1.0]])
    prolong = np.kron(np.kron(ramp_basis, ramp_basis), ramp_basis)
    coarse_stiff = prolong.T @ stiffness @ prolong
    small_mass = ramp_basis.T @ ramp_basis
    face_mass = np.kron(small_mass, small_mass)
    return (stiffness, prolong, coarse_stiff, face_mass)


def face_slices(points):
    grid_ids = np.arange(points**3).reshape(points, points, points)
    last_index = points - 1
    return [
        grid_ids[0],
        grid_ids[last_index],
        grid_ids[:, 0],
        grid_ids[:, last_index],
        grid_ids[:, :, 0],
        grid_ids[:, :, last_index],
    ]


def lifting(points, face_mat):
    node_total = points**3
    per_face = points * points
    slices = face_slices(points)
    result = np.zeros((node_total, 6 * per_face))
    for face in range(6):
        select = np.zeros((node_total, per_face))
        select[slices[face].ravel(), np.arange(per_face)] = 1.0
        result[:, face * per_face : (face + 1) * per_face] = PENALTY * (select @ face_mat)
    return result


def face_diagonal(points, face_mat):
    result = np.zeros(points**3)
    for face_ids in face_slices(points):
        result[face_ids.ravel()] += PENALTY * main_diagonal(face_mat)
    return result


def stiff_and_traces(stiff, points):
    node_total = points**3
    per_face = points * points
    select = np.zeros((6 * per_face, node_total))
    for face, ids in enumerate(face_slices(points)):
        select[face * per_face + np.arange(per_face), ids.ravel()] = 1.0
    return np.concatenate([stiff, select], axis=0)


def shift_columns(values, offset):
    rows, width = values.shape
    pad = jnp.zeros((rows, abs(offset)), values.dtype)
    if offset > 0:
        return jnp.concatenate([values[:, offset:], pad], axis=1)
    return jnp.concatenate([pad, values[:, : width + offset]], axis=1)


def snake_places(mesh_size, inner_size, y_size=4, cores=2):
    places = np.zeros(mesh_size * inner_size, np.int64)
    for slab in range(mesh_size * inner_size):
        row, inner = divmod(slab, inner_size)
        z, rest = divmod(row, y_size * cores)
        y, core = divmod(rest, cores)
        x_place = inner if core % 2 == 0 else inner_size - 1 - inner
        y_place = y if z % 2 == 0 else y_size - 1 - y
        places[slab] = ((z * y_size + y_place) * cores + core) * inner_size + x_place
    return places


def scale_of(level):
    return 96.0 * PENALTY * (8.0 * 2.0**level) ** (2.0 / 3.0)


def local(source, density, neighbours, halo_sends, aggregate, partner_map):
    stiffness, prolong, coarse_stiff, face_mass = build_tables()
    big_fine = jnp.asarray(stiff_and_traces(stiffness, 4), jnp.float32)
    big_lin = jnp.asarray(stiff_and_traces(coarse_stiff, 2), jnp.float32)
    prolong_mat = jnp.asarray(prolong, jnp.float32)
    lift_fine = jnp.asarray(lifting(4, np.eye(16)), jnp.float32)
    lift_lin = jnp.asarray(lifting(2, face_mass), jnp.float32)
    diag_fine_k = jnp.asarray(main_diagonal(stiffness), jnp.float32)
    diag_fine_f = jnp.asarray(face_diagonal(4, np.eye(16)), jnp.float32)
    diag_lin_k = jnp.asarray(main_diagonal(coarse_stiff), jnp.float32)
    diag_lin_f = jnp.asarray(face_diagonal(2, face_mass), jnp.float32)
    elements = source.shape[1]
    layer = halo_sends.shape[1]
    groups_width = elements // 8

    ordering = jnp.concatenate([halo_sends[0], halo_sends[1]])
    to_brick = (
        jnp.arange(elements, dtype=jnp.int32)[:, None] == ordering[None, :]
    ).astype(jnp.float32)
    stacked_inputs = jnp.concatenate(
        [source, density[None, :], aggregate.astype(jnp.float32)[None, :]], axis=0
    )
    bundle = jnp.dot(stacked_inputs, to_brick, precision=PRECISE)

    devices = lax.axis_size("mesh") * lax.axis_size("inner")
    places = snake_places(lax.axis_size("mesh"), lax.axis_size("inner"))
    slab_of = np.argsort(places)
    here = lax.axis_index("mesh") * lax.axis_size("inner") + lax.axis_index("inner")
    flat_index = jnp.asarray(slab_of, jnp.int32)[here]
    bundle = lax.ppermute(bundle, AXES, [(q, int(places[q])) for q in range(devices)])
    (
        big_fine, big_lin, prolong_mat, lift_fine, lift_lin,
        diag_fine_k, diag_fine_f, diag_lin_k, diag_lin_f, partner_map,
    ) = lax.optimization_barrier((
        big_fine, big_lin, prolong_mat, lift_fine, lift_lin,
        diag_fine_k, diag_fine_f, diag_lin_k, diag_lin_f, partner_map,
    ))
    rhs = bundle[:-2]
    dens = bundle[-2]
    agg = jnp.round(bundle[-1]).astype(jnp.int32)
    up_pairs = [(int(places[d]), int(places[d + 1])) for d in range(devices - 1)]
    down_pairs = [(b, a) for a, b in up_pairs]

    last_x = layer // BRICK_Y - 1
    runtime_zero = lax.optimization_barrier(jnp.zeros((), jnp.int32))

    def wall_masks(width):
        column = lax.broadcasted_iota(jnp.int32, (1, width), 1) + runtime_zero
        pos_x = column % layer // BRICK_Y
        pos_y = column % BRICK_Y
        return [pos_x > 0, pos_x < last_x, pos_y > 0, pos_y < BRICK_Y - 1]

    masks = wall_masks(elements)
    offsets = [-BRICK_Y, BRICK_Y, -1, 1]

    diag_fine = dens[None, :] * diag_fine_k[:, None] + diag_fine_f[:, None]
    diag_lin = dens[None, :] * diag_lin_k[:, None] + diag_lin_f[:, None]

    def apply(nodal_field, big, lift, node_total, per_face):
        stacked = jnp.dot(big, nodal_field, precision=PRECISE)
        stiff_part = stacked[:node_total]
        traces = [
            stacked[node_total + f * per_face : node_total + (f + 1) * per_face] for f in range(6)
        ]
        rim_low = lax.ppermute(traces[5][:, layer:], AXES, up_pairs)
        rim_high = lax.ppermute(traces[4][:, :layer], AXES, down_pairs)
        jumps = []
        for face in range(4):
            other = shift_columns(traces[face ^ 1], offsets[face])
            jumps.append(traces[face] - jnp.where(masks[face], other, 0.0))
        jumps.append(traces[4] - jnp.concatenate([rim_low, traces[5][:, :layer]], axis=1))
        jumps.append(traces[5] - jnp.concatenate([traces[4][:, layer:], rim_high], axis=1))
        jumps = jnp.concatenate(jumps, axis=0)
        return dens[None, :] * stiff_part + jnp.dot(lift, jumps, precision=PRECISE)

    wide_masks = wall_masks(3 * elements)

    def apply_wide(nodal_field, wide_dens, big=None, lift=None, node_total=8, per_face=4):
        big = big_lin if big is None else big
        lift = lift_lin if lift is None else lift
        stacked = jnp.dot(big, nodal_field, precision=PRECISE)
        stiff_part = stacked[:node_total]
        traces = [
            stacked[node_total + f * per_face : node_total + (f + 1) * per_face] for f in range(6)
        ]
        jumps = []
        for face in range(4):
            other = shift_columns(traces[face ^ 1], offsets[face])
            jumps.append(traces[face] - jnp.where(wide_masks[face], other, 0.0))
        jumps.append(traces[4] - shift_columns(traces[5], -layer))
        jumps.append(traces[5] - shift_columns(traces[4], layer))
        jumps = jnp.concatenate(jumps, axis=0)
        return wide_dens[None, :] * stiff_part + jnp.dot(lift, jumps, precision=PRECISE)

    def apply_fine(nodal_field):
        return apply(nodal_field, big_fine, lift_fine, 64, 16)

    def apply_lin(nodal_field):
        return apply(nodal_field, big_lin, lift_lin, 8, 4)

    assert SMOOTH_FINE - 1 <= 2
    own = slice(elements, 2 * elements)
    keep = jnp.concatenate(
        [
            jnp.full((elements,), flat_index > 0),
            jnp.ones((elements,), bool),
            jnp.full((elements,), flat_index < devices - 1),
        ]
    )[None, :]
    fine_slab = jnp.concatenate([rhs, dens[None, :]], axis=0)
    below_fine = lax.ppermute(fine_slab, AXES, up_pairs)
    above_fine = lax.ppermute(fine_slab, AXES, down_pairs)
    wide_rhs = jnp.concatenate([below_fine[:-1], rhs, above_fine[:-1]], axis=1)
    wide_dens_fine = jnp.concatenate([below_fine[-1], dens, above_fine[-1]])
    wide_diag_fine = wide_dens_fine[None, :] * diag_fine_k[:, None] + diag_fine_f[:, None]
    wide = jnp.where(keep, FINE_WEIGHT * wide_rhs / wide_diag_fine, 0.0)
    for sweep in range(SMOOTH_FINE - 1):
        wide_applied = apply_wide(wide, wide_dens_fine, big_fine, lift_fine, 64, 16)
        wide = wide + FINE_WEIGHT * (wide_rhs - wide_applied) / wide_diag_fine
        wide = jnp.where(keep, wide, 0.0)
    solution = wide[:, own]
    resid_fine = rhs - apply_fine(solution)
    resid_lin = jnp.dot(prolong_mat.T, resid_fine, precision=PRECISE)
    assert SMOOTH_LIN <= 2
    slab = jnp.concatenate([resid_lin, dens[None, :]], axis=0)
    below = lax.ppermute(slab, AXES, up_pairs)
    above = lax.ppermute(slab, AXES, down_pairs)
    wide_resid = jnp.concatenate([below[:-1], resid_lin, above[:-1]], axis=1)
    wide_dens = jnp.concatenate([below[-1], dens, above[-1]])
    wide_diag = wide_dens[None, :] * diag_lin_k[:, None] + diag_lin_f[:, None]
    wide = LINEAR_WEIGHT * wide_resid / wide_diag
    for sweep in range(SMOOTH_LIN - 1):
        wide = wide + LINEAR_WEIGHT * (wide_resid - apply_wide(wide, wide_dens)) / wide_diag
        wide = jnp.where(keep, wide, 0.0)
    left_lin = resid_lin - apply_wide(wide, wide_dens)[:, own]
    linear = wide[:, own]
    resid_elem = jnp.sum(left_lin, axis=0)

    group_ids = jnp.arange(groups_width, dtype=jnp.int32)
    agg_hot = agg[:, None] == group_ids[None, :]
    own_sums = jnp.sum(jnp.where(agg_hot, resid_elem[:, None], 0.0), axis=0)

    current = own_sums
    descent = []
    level = 0
    while 2**level < devices:
        pairs = [(int(places[d]), int(places[d ^ (1 << level)])) for d in range(devices)]
        partner = lax.ppermute(current, AXES, pairs)
        below_term = current / scale_of(level)
        is_lower = (flat_index >> level) % 2 == 0
        paired = jnp.where(
            is_lower, jnp.concatenate([current, partner]), jnp.concatenate([partner, current])
        )
        level += 1
        row_index = flat_index // 2**level * 2**level + (2 ** (level - 1) - 1)
        parents = lax.dynamic_index_in_dim(partner_map, row_index, 0, keepdims=False)
        hot = parents[:, None] == group_ids[None, :]
        current = jnp.sum(jnp.where(hot, paired[:, None], 0.0), axis=0)
        descent.append((hot, is_lower, below_term))
    total = current / scale_of(level)
    for hot, is_lower, below_term in reversed(descent):
        children = jnp.sum(jnp.where(hot, total[None, :], 0.0), axis=1)
        total = (
            jnp.where(is_lower, children[:groups_width], children[groups_width:]) + below_term
        )
    own_total = total
    coarse = resid_elem / (96.0 * PENALTY) + jnp.sum(
        jnp.where(agg_hot, own_total[None, :], 0.0), axis=1
    )

    linear = linear + coarse[None, :]
    wide = jnp.concatenate(
        [
            lax.ppermute(linear, AXES, up_pairs),
            linear,
            lax.ppermute(linear, AXES, down_pairs),
        ],
        axis=1,
    )
    for sweep in range(SMOOTH_LIN):
        wide = wide + LINEAR_WEIGHT * (wide_resid - apply_wide(wide, wide_dens)) / wide_diag
        wide = jnp.where(keep, wide, 0.0)
    linear = wide[:, own]
    solution = solution + jnp.dot(prolong_mat, linear, precision=PRECISE)
    wide = jnp.concatenate(
        [
            lax.ppermute(solution, AXES, up_pairs),
            solution,
            lax.ppermute(solution, AXES, down_pairs),
        ],
        axis=1,
    )
    for sweep in range(SMOOTH_FINE - 1):
        wide_applied = apply_wide(wide, wide_dens_fine, big_fine, lift_fine, 64, 16)
        wide = wide + FINE_WEIGHT * (wide_rhs - wide_applied) / wide_diag_fine
        wide = jnp.where(keep, wide, 0.0)
    solution = wide[:, own]
    solution = solution + FINE_WEIGHT * (rhs - apply_fine(solution)) / diag_fine
    result = jnp.concatenate([solution, coarse[None, :]], axis=0)
    result = lax.ppermute(result, AXES, [(int(places[d]), d) for d in range(devices)])
    result = lax.dot_general(
        result, to_brick, (((1,), (1,)), ((), ())), precision=PRECISE
    )
    return (result[:-1], result[-1])


def solution(mesh):
    return jax.shard_map(
        local,
        mesh=mesh,
        in_specs=(
            P(None, ("mesh", "inner")),
            P(("mesh", "inner")),
            P(None, ("mesh", "inner")),
            P(None, ("mesh", "inner")),
            P(("mesh", "inner")),
            P(),
        ),
        out_specs=(P(None, ("mesh", "inner")), P(("mesh", "inner"))),
        check_vma=False,
    )
```
